256 devices in a mesh: row: 8 (over y, core), col: 32 (over z, x).
Axes of the slice: x: 4, y: 4, z: 8, core: 2. Of those that a mesh axis runs over, the one named last changes fastest.
Arguments:
- blocks: float32 [128, 32, 256, 256], P('row', 'col'), may hold values from -6 to 6
- panel_rows: int32 [2, 64], P(None, 'row'), may hold values from -1 to 767, as said below
- target_slots: int32 [2, 128, 32], P(None, 'row', 'col'), may hold values from -1 to 7, as said below
- diag_inverse: float32 [2, 256, 256], replicated, may hold values from -1 to 1, as said below
- cross_block: float32 [256, 256], replicated, may hold values from -6 to 6
Outputs:
- factored: float32 [128, 32, 256, 256], P('row', 'col')
The draws below stay inside these ranges and needn't reach their ends.
Inputs may be any that keep to these rules, and one draw needn't show every extreme that they name: `panel_rows`: slot q * 2 + m of row device r stands for the m-th structure row of block column class r + q times the number of row devices; both lists are -1 where that class is 0 or 1, and list 0 is -1 also where block column 0 lacks the row; otherwise list 0 equals list 1. `target_slots`: A filled slot of class c names in entry 0 a slot of its own row device and in entry 1 a slot of row device c modulo the number of row devices, within (c // number of row devices) * 2 and the 1 after it; both are filled or both -1, always -1 in classes 0 and 1; the target's block row number is at least its block column number. `diag_inverse`: each matrix is lower triangular.
All inputs are finite; a program needn't handle non-finite values.
Results may differ from the reference program's by a relative error of at most 0.0003.
Values sent between devices are 32-bit elements; how exact they have to be, the bound alone decides.
No kernel may reach another device: no remote copies, remote signals or barrier semaphores. Data moves between devices by JAX's collectives and lax.ppermute only.
A program may use at most 128 MiB of HBM per device.

```python
import math
import jax
import jax.numpy as jnp
from jax import lax

BLOCK = 256
PER_CLASS = 2
GROUPS = 24
PANEL_SLOTS = 8
SLOTS = 16
N_ROW = 8
N_COL = 32


def structure(key):
    base_key = jax.random.fold_in(key, 17)
    member_keys = jax.random.split(jax.random.fold_in(base_key, 1), N_COL)
    members = jax.vmap(lambda member_key: jax.random.permutation(member_key, GROUPS)[:PER_CLASS])(member_keys).astype(jnp.int32)
    classes = jnp.arange(N_COL, dtype=jnp.int32)
    block_row = classes[:, None] + N_COL * members
    per_row = N_COL // N_ROW
    owner_class = jnp.arange(N_ROW, dtype=jnp.int32)[:, None] + N_ROW * jnp.arange(per_row, dtype=jnp.int32)[None, :]
    rows_panel = block_row[owner_class]
    valid_slot = (owner_class >= 2)[:, :, None]
    second_rows = jnp.where(valid_slot, rows_panel, -1).reshape(N_ROW, PANEL_SLOTS)
    kept_rows = jax.random.randint(jax.random.fold_in(base_key, 2), (N_ROW, PANEL_SLOTS), 0, 5) < 3
    first_rows = jnp.where(kept_rows & (second_rows >= 0), second_rows, -1)
    live_pairs = (second_rows[:, None, :, None] >= 0) & (second_rows[:, None, :, None] >= block_row[None, :, None, :]) & (classes >= 2)[None, :, None, None]
    live_pairs = live_pairs.reshape(N_ROW, N_COL, SLOTS)
    rank_keys = jax.random.split(jax.random.fold_in(base_key, 3), N_ROW * N_COL)
    rank_order = jax.vmap(lambda member_key: jax.random.permutation(member_key, SLOTS))(rank_keys).astype(jnp.int32).reshape(N_ROW, N_COL, SLOTS)
    scores = jnp.where(live_pairs, 0, SLOTS).astype(jnp.int32) + rank_order
    sort_order = jnp.argsort(scores, axis=-1, stable=True).astype(jnp.int32)
    chosen_live = jnp.take_along_axis(live_pairs, sort_order, axis=-1)
    row_slot = jnp.where(chosen_live, sort_order // PER_CLASS, -1)
    col_slot = jnp.where(chosen_live, (classes // N_ROW)[None, :, None] * PER_CLASS + sort_order % PER_CLASS, -1)
    target_table = jnp.stack([row_slot, col_slot]).transpose(0, 1, 3, 2).reshape(2, N_ROW * SLOTS, N_COL).astype(jnp.int32)
    panel_table = jnp.stack([first_rows, second_rows]).reshape(2, N_ROW * PANEL_SLOTS).astype(jnp.int32)
    return (panel_table, target_table)


def draw_panel_rows(key, part):
    return structure(key)[0]


def draw_target_slots(key, part):
    return structure(key)[1]


def draw_diag_inverse(key, part):
    base_key = jax.random.fold_in(key, 29)
    lower_key, diag_key = jax.random.split(base_key)
    block_shape = (2, BLOCK, BLOCK)
    lower = jax.random.normal(lower_key, block_shape, jnp.float32)
    diagonal = jax.random.uniform(diag_key, (2, BLOCK), jnp.float32, 0.5, 1.0)
    positions = jnp.arange(BLOCK)
    below = positions[:, None] > positions[None, :]
    on_diagonal = positions[:, None] == positions[None, :]
    return 0.3 * (jnp.where(below, lower * (0.8 / math.sqrt(BLOCK)), 0.0) + jnp.where(on_diagonal, diagonal[:, :, None], 0.0))


def block_levels(key, shape, pieces, low, top_value):
    factor_of = 1.0
    for position, parts in pieces:
        draws = jax.random.uniform(jax.random.fold_in(jax.random.fold_in(key, 6), position), (parts,), jnp.float32, low / len(pieces), top_value / len(pieces))
        factor_of = factor_of * jnp.repeat(jnp.exp(draws), shape[position] // parts).reshape((-1,) + (1,) * (len(shape) - 1 - position))
    return factor_of


def centred(rng, dims, width, bound, cuts=(), kind=jnp.bfloat16):
    values = width * jax.random.normal(rng, dims, jnp.float32)
    if cuts:
        values = values * block_levels(rng, dims, cuts, -0.22, 0.18)
    return jnp.clip(values, -bound, bound).astype(kind)


def setup_inputs(seed: int = 0) -> dict:
    keys = jax.random.split(jax.random.key(seed), 6)
    return {
        "blocks": centred(keys[0], (N_ROW * SLOTS, N_COL, BLOCK, BLOCK), 1.0, 6.0, ((0, 8), (1, 32)), jnp.float32),
        "panel_rows": draw_panel_rows(jax.random.fold_in(keys[5], 71), 0),
        "target_slots": draw_target_slots(jax.random.fold_in(keys[5], 71), 0),
        "diag_inverse": draw_diag_inverse(jax.random.fold_in(keys[5], 71), 0),
        "cross_block": centred(keys[4], (BLOCK, BLOCK), 1.0, 6.0, (), jnp.float32),
    }


HIGHEST_PRECISION = lax.Precision.HIGHEST


def reference(blocks, panel_rows, target_slots, diag_inverse, cross_block):
    block_grid = blocks.reshape(N_ROW, SLOTS, N_COL, BLOCK, BLOCK)
    first_live = (panel_rows[0] >= 0).reshape(N_ROW, PANEL_SLOTS)[:, :, None, None]
    second_live = (panel_rows[1] >= 0).reshape(N_ROW, PANEL_SLOTS)[:, :, None, None]
    cross_factor = jnp.dot(cross_block, diag_inverse[0].T, precision=HIGHEST_PRECISION)
    head_zero = block_grid[:, :PANEL_SLOTS, 0]
    head_one = block_grid[:, :PANEL_SLOTS, 1]
    first_factor = jnp.where(first_live, jnp.einsum("rsab,cb->rsac", head_zero, diag_inverse[0], precision=HIGHEST_PRECISION), 0.0)
    updated = head_one - jnp.einsum("rsab,cb->rsac", first_factor, cross_factor, precision=HIGHEST_PRECISION)
    second_factor = jnp.where(second_live, jnp.einsum("rsab,cb->rsac", updated, diag_inverse[1], precision=HIGHEST_PRECISION), 0.0)
    both_factors = jnp.concatenate([first_factor, second_factor], axis=3)
    slot_table = target_slots.reshape(2, N_ROW, SLOTS, N_COL)
    class_rows = jnp.arange(N_COL, dtype=jnp.int32) % N_ROW

    def one_row(device_row):
        row_index = slot_table[0, device_row]
        col_index = slot_table[1, device_row]
        present = row_index >= 0
        left_blocks = both_factors[device_row][jnp.where(present, row_index, 0)]
        right_blocks = both_factors[class_rows[None, :], jnp.where(present, col_index, 0)]
        schur_term = jnp.einsum("scak,scbk->scab", left_blocks, right_blocks, precision=HIGHEST_PRECISION)
        stored = block_grid[device_row]
        result = stored - jnp.where(present[:, :, None, None], schur_term, 0.0)
        result = result.at[:PANEL_SLOTS, 0].set(jnp.where(first_live[device_row], first_factor[device_row], result[:PANEL_SLOTS, 0]))
        result = result.at[:PANEL_SLOTS, 1].set(jnp.where(second_live[device_row], second_factor[device_row], result[:PANEL_SLOTS, 1]))
        return result

    factored = lax.map(one_row, jnp.arange(N_ROW, dtype=jnp.int32))
    return factored.reshape(blocks.shape)
```

```python
import jax
import jax.numpy as jnp
from jax import lax
from jax.sharding import PartitionSpec as P

PER_CLASS = 2


HIGHEST_PRECISION = lax.Precision.HIGHEST


def broadcast(array, axis, root):
    mine = lax.axis_index(axis) == root
    return lax.psum(jnp.where(mine, array, jnp.zeros_like(array)), axis)


def apply_inverse(panel_rows_block, inverse):
    return jnp.einsum("ab,cb->ac", panel_rows_block, inverse, precision=HIGHEST_PRECISION)


def per_device(blocks, panel_rows, target_slots, diag_inverse, cross_block):
    column = lax.axis_index("col")
    row_count = lax.axis_size("row")
    col_count = lax.axis_size("col")
    stored = blocks[:, 0]
    slot_count = panel_rows.shape[1]
    block = stored.shape[-1]
    head_part = stored[:slot_count]
    chunk = slot_count * block // col_count
    pieces = head_part.reshape(col_count, chunk, block)
    received = lax.all_to_all(pieces, "col", 0, 0, tiled=True)
    zero_rows = received[0]
    one_rows = received[1]
    piece_slot = column * chunk // block
    first_live = lax.dynamic_index_in_dim(panel_rows[0], piece_slot, keepdims=False) >= 0
    second_live = lax.dynamic_index_in_dim(panel_rows[1], piece_slot, keepdims=False) >= 0
    cross_factor = jnp.dot(cross_block, diag_inverse[0].T, precision=HIGHEST_PRECISION)
    first_piece = jnp.where(first_live, apply_inverse(zero_rows, diag_inverse[0]), 0.0)
    updated_piece = one_rows - apply_inverse(first_piece, cross_factor)
    second_piece = jnp.where(second_live, apply_inverse(updated_piece, diag_inverse[1]), 0.0)
    both_pieces = jnp.stack([first_piece, second_piece])
    both_rows = lax.all_gather(both_pieces, "col", axis=1, tiled=True)
    both_rows = both_rows.reshape(2, slot_count, block, block)
    first_rows = both_rows[0]
    second_rows = both_rows[1]
    class_start = column // row_count * PER_CLASS
    owner_row = column % row_count
    both_cols = broadcast(
        lax.dynamic_slice_in_dim(both_rows, class_start, PER_CLASS, 1), "row", owner_row
    )
    first_cols = both_cols[0]
    second_cols = both_cols[1]
    row_index = target_slots[0, :, 0]
    col_index = target_slots[1, :, 0]
    present = row_index >= 0
    left_slot = jnp.where(present, row_index, 0)
    right_slot = jnp.where(present, col_index - class_start, 0)
    left_blocks = jnp.concatenate([first_rows[left_slot], second_rows[left_slot]], axis=2)
    right_blocks = jnp.concatenate([first_cols[right_slot], second_cols[right_slot]], axis=2)
    schur_term = jnp.einsum("sak,sbk->sab", left_blocks, right_blocks, precision=HIGHEST_PRECISION)
    trailing = stored - jnp.where(present[:, None, None], schur_term, 0.0)
    head_live = panel_rows >= 0
    keep_mask = ((column == 0) & head_live[0] | (column == 1) & head_live[1])[:, None, None]
    own_panel = jnp.where(column == 0, first_rows, second_rows)
    head_blocks = jnp.where(keep_mask, own_panel, trailing[:slot_count])
    factored = jnp.concatenate([head_blocks, trailing[slot_count:]], axis=0)
    return factored[:, None]


def solution(mesh):
    return jax.shard_map(
        per_device,
        mesh=mesh,
        in_specs=(P("row", "col", None, None), P(None, "row"), P(None, "row", "col"), P(), P()),
        out_specs=P("row", "col", None, None),
        check_vma=False,
    )
```

```python
import jax
import jax.numpy as jnp
import numpy as np
from jax import lax
from jax.sharding import Mesh
from jax.sharding import PartitionSpec as P

PER_CLASS = 2
X_SIZE = 4


HIGHEST_PRECISION = lax.Precision.HIGHEST
COL_AXES = ("zh", "zl", "x")
CLASS_AXES = ("zl", "x")


def apply_inverse(panel_rows_block, inverse):
    return jnp.einsum("ab,cb->ac", panel_rows_block, inverse, precision=HIGHEST_PRECISION)


def per_device(blocks, panel_rows, target_slots, diag_inverse, cross_block):
    row_count = lax.axis_size("row")
    col_count = lax.axis_size(COL_AXES)
    column = lax.axis_index(COL_AXES)
    stored = blocks[:, 0]
    slot_count = panel_rows.shape[1]
    block = stored.shape[-1]
    head_part = stored[:slot_count]
    chunk = slot_count * block // col_count
    pieces = head_part.reshape(col_count, chunk, block)
    received = lax.all_to_all(pieces, COL_AXES, 0, 0, tiled=True)
    zero_rows = received[0]
    one_rows = received[1]
    piece_slot = column * chunk // block
    first_live = lax.dynamic_index_in_dim(panel_rows[0], piece_slot, keepdims=False) >= 0
    second_live = lax.dynamic_index_in_dim(panel_rows[1], piece_slot, keepdims=False) >= 0
    cross_factor = jnp.dot(cross_block, diag_inverse[0].T, precision=HIGHEST_PRECISION)
    first_piece = jnp.where(first_live, apply_inverse(zero_rows, diag_inverse[0]), 0.0)
    updated_piece = one_rows - apply_inverse(first_piece, cross_factor)
    second_piece = jnp.where(second_live, apply_inverse(updated_piece, diag_inverse[1]), 0.0)
    both_pieces = jnp.stack([first_piece, second_piece])
    class_size = lax.axis_size(CLASS_AXES)
    swap = [(a * class_size + b, b * class_size + a) for a in range(row_count) for b in range(class_size)]
    swapped = lax.ppermute(both_pieces, ("row",) + CLASS_AXES, swap)
    class_pieces = lax.all_gather(swapped, "row", axis=0, tiled=False)
    per_slot = block // chunk
    class_pieces = class_pieces.reshape(PER_CLASS, per_slot, 2, chunk, block)
    both_cols = class_pieces.transpose(2, 0, 1, 3, 4).reshape(2, PER_CLASS, block, block)
    both_rows = lax.all_gather(both_pieces, "x", axis=1, tiled=True)
    both_rows = lax.all_gather(both_rows, ("zh", "zl"), axis=1, tiled=True)
    both_rows = both_rows.reshape(2, slot_count, block, block)
    first_rows = both_rows[0]
    second_rows = both_rows[1]
    first_cols = both_cols[0]
    second_cols = both_cols[1]
    class_start = column // row_count * PER_CLASS
    row_index = target_slots[0, :, 0]
    col_index = target_slots[1, :, 0]
    present = row_index >= 0
    left_slot = jnp.where(present, row_index, 0)
    right_slot = jnp.where(present, col_index - class_start, 0)
    left_blocks = jnp.concatenate([first_rows[left_slot], second_rows[left_slot]], axis=2)
    right_blocks = jnp.concatenate([first_cols[right_slot], second_cols[right_slot]], axis=2)
    schur_term = jnp.einsum("sak,sbk->sab", left_blocks, right_blocks, precision=HIGHEST_PRECISION)
    trailing = stored - jnp.where(present[:, None, None], schur_term, 0.0)
    head_live = panel_rows >= 0
    keep_mask = ((column == 0) & head_live[0] | (column == 1) & head_live[1])[:, None, None]
    own_panel = jnp.where(column == 0, first_rows, second_rows)
    head_blocks = jnp.where(keep_mask, own_panel, trailing[:slot_count])
    factored = jnp.concatenate([head_blocks, trailing[slot_count:]], axis=0)
    return factored[:, None]


def solution(mesh):
    row_count = mesh.shape["row"]
    col_count = mesh.shape["col"]
    devices = np.asarray(mesh.devices).reshape(
        row_count, col_count // row_count, row_count // X_SIZE, X_SIZE
    )
    split_mesh = Mesh(devices, ("row",) + COL_AXES)
    return jax.shard_map(
        per_device,
        mesh=split_mesh,
        in_specs=(
            P("row", COL_AXES, None, None),
            P(None, "row"),
            P(None, "row", COL_AXES),
            P(),
            P(),
        ),
        out_specs=P("row", COL_AXES, None, None),
        check_vma=False,
    )
```

```python
import jax
import jax.numpy as jnp
import numpy as np
from jax import lax
from jax.sharding import Mesh
from jax.sharding import PartitionSpec as P

PER_CLASS = 2
X_SIZE = 4


HIGHEST_PRECISION = lax.Precision.HIGHEST
PRODUCT_PRECISION = lax.Precision.HIGH
COL_AXES = ("zh", "zl", "x")
CLASS_AXES = ("zl", "x")


def apply_inverse(panel_rows_block, inverse):
    return jnp.einsum("ab,cb->ac", panel_rows_block, inverse, precision=HIGHEST_PRECISION)


def per_device(blocks, panel_rows, target_slots, diag_inverse, cross_block):
    row_count = lax.axis_size("row")
    col_count = lax.axis_size(COL_AXES)
    column = lax.axis_index(COL_AXES)
    stored = blocks[:, 0]
    slot_count = panel_rows.shape[1]
    block = stored.shape[-1]
    head_part = stored[:slot_count]
    chunk = slot_count * block // col_count
    pieces = head_part.reshape(col_count, chunk, block)
    received = lax.all_to_all(pieces, COL_AXES, 0, 0, tiled=True)
    zero_rows = received[0]
    one_rows = received[1]
    piece_slot = column * chunk // block
    first_live = lax.dynamic_index_in_dim(panel_rows[0], piece_slot, keepdims=False) >= 0
    second_live = lax.dynamic_index_in_dim(panel_rows[1], piece_slot, keepdims=False) >= 0
    cross_factor = jnp.dot(cross_block, diag_inverse[0].T, precision=HIGHEST_PRECISION)
    first_piece = jnp.where(first_live, apply_inverse(zero_rows, diag_inverse[0]), 0.0)
    updated_piece = one_rows - apply_inverse(first_piece, cross_factor)
    second_piece = jnp.where(second_live, apply_inverse(updated_piece, diag_inverse[1]), 0.0)
    both_pieces = jnp.stack([first_piece, second_piece])
    class_size = lax.axis_size(CLASS_AXES)
    swap = [(a * class_size + b, b * class_size + a) for a in range(row_count) for b in range(class_size)]
    swapped = lax.ppermute(both_pieces, ("row",) + CLASS_AXES, swap)
    class_pieces = lax.all_gather(swapped, "row", axis=0, tiled=False)
    per_slot = block // chunk
    class_pieces = class_pieces.reshape(PER_CLASS, per_slot, 2, chunk, block)
    both_cols = class_pieces.transpose(2, 0, 1, 3, 4).reshape(2, PER_CLASS, block, block)
    both_rows = lax.all_gather(both_pieces, "x", axis=1, tiled=True)
    both_rows = lax.all_gather(both_rows, ("zh", "zl"), axis=1, tiled=True)
    both_rows = both_rows.reshape(2, slot_count, block, block)
    first_rows = both_rows[0]
    second_rows = both_rows[1]
    class_start = column // row_count * PER_CLASS
    row_index = target_slots[0, :, 0]
    col_index = target_slots[1, :, 0]
    present = row_index >= 0
    left_slot = jnp.where(present, row_index, 0)
    right_slot = jnp.where(present, col_index - class_start, 0)
    products = jnp.einsum("fakm,fbjm->abkj", both_rows, both_cols, precision=PRODUCT_PRECISION)
    products = products.reshape(slot_count * PER_CLASS, block, block)
    schur_term = products[left_slot * PER_CLASS + right_slot]
    trailing = stored - jnp.where(present[:, None, None], schur_term, 0.0)
    head_live = panel_rows >= 0
    keep_mask = ((column == 0) & head_live[0] | (column == 1) & head_live[1])[:, None, None]
    own_panel = jnp.where(column == 0, first_rows, second_rows)
    head_blocks = jnp.where(keep_mask, own_panel, trailing[:slot_count])
    factored = jnp.concatenate([head_blocks, trailing[slot_count:]], axis=0)
    return factored[:, None]


def solution(mesh):
    row_count = mesh.shape["row"]
    col_count = mesh.shape["col"]
    devices = np.asarray(mesh.devices).reshape(
        row_count, col_count // row_count, row_count // X_SIZE, X_SIZE
    )
    split_mesh = Mesh(devices, ("row",) + COL_AXES)
    return jax.shard_map(
        per_device,
        mesh=split_mesh,
        in_specs=(
            P("row", COL_AXES, None, None),
            P(None, "row"),
            P(None, "row", COL_AXES),
            P(),
            P(),
        ),
        out_specs=P("row", COL_AXES, None, None),
        check_vma=False,
    )
```

```python
import jax
import jax.numpy as jnp
import numpy as np
from jax import lax
from jax.sharding import Mesh
from jax.sharding import PartitionSpec as P

PER_CLASS = 2
X_SIZE = 4


HIGHEST_PRECISION = lax.Precision.HIGHEST
PRODUCT_PRECISION = lax.Precision.HIGH
COL_AXES = ("zh", "zl", "x")
CLASS_AXES = ("zl", "x")


def apply_inverse(panel_rows_block, inverse):
    return jnp.einsum("ab,cb->ac", panel_rows_block, inverse, precision=HIGHEST_PRECISION)


def per_device(blocks, panel_rows, target_slots, diag_inverse, cross_block):
    row_count = lax.axis_size("row")
    col_count = lax.axis_size(COL_AXES)
    column = lax.axis_index(COL_AXES)
    stored = blocks[:, 0]
    slot_count = panel_rows.shape[1]
    block = stored.shape[-1]
    head_part = stored[:slot_count]
    chunk = slot_count * block // col_count
    pieces = head_part.reshape(col_count, chunk, block)
    received = lax.all_to_all(pieces, COL_AXES, 0, 0, tiled=True)
    zero_rows = received[0]
    one_rows = received[1]
    piece_slot = column * chunk // block
    first_live = lax.dynamic_index_in_dim(panel_rows[0], piece_slot, keepdims=False) >= 0
    second_live = lax.dynamic_index_in_dim(panel_rows[1], piece_slot, keepdims=False) >= 0
    cross_factor = jnp.dot(cross_block, diag_inverse[0].T, precision=HIGHEST_PRECISION)
    first_piece = jnp.where(first_live, apply_inverse(zero_rows, diag_inverse[0]), 0.0)
    updated_piece = one_rows - apply_inverse(first_piece, cross_factor)
    second_piece = jnp.where(second_live, apply_inverse(updated_piece, diag_inverse[1]), 0.0)
    both_pieces = jnp.stack([first_piece, second_piece])
    class_size = lax.axis_size(CLASS_AXES)
    swap = [(a * class_size + b, b * class_size + a) for a in range(row_count) for b in range(class_size)]
    swapped = lax.ppermute(both_pieces, ("row",) + CLASS_AXES, swap)
    spread = jnp.broadcast_to(swapped[None], (row_count,) + swapped.shape)
    class_pieces = lax.all_to_all(spread, "row", 0, 0, tiled=True)
    per_slot = block // chunk
    class_pieces = class_pieces.reshape(PER_CLASS, per_slot, 2, chunk, block)
    both_cols = class_pieces.transpose(2, 0, 1, 3, 4).reshape(2, PER_CLASS, block, block)
    both_rows = lax.all_gather(both_pieces, "x", axis=1, tiled=True)
    both_rows = lax.all_gather(both_rows, ("zh", "zl"), axis=1, tiled=True)
    both_rows = both_rows.reshape(2, slot_count, block, block)
    first_rows = both_rows[0]
    second_rows = both_rows[1]
    class_start = column // row_count * PER_CLASS
    row_index = target_slots[0, :, 0]
    col_index = target_slots[1, :, 0]
    present = row_index >= 0
    left_slot = jnp.where(present, row_index, 0)
    right_slot = jnp.where(present, col_index - class_start, 0)
    products = jnp.einsum("fakm,fbjm->abkj", both_rows, both_cols, precision=PRODUCT_PRECISION)
    products = products.reshape(slot_count * PER_CLASS, block, block)
    schur_term = products[left_slot * PER_CLASS + right_slot]
    trailing = stored - jnp.where(present[:, None, None], schur_term, 0.0)
    head_live = panel_rows >= 0
    keep_mask = ((column == 0) & head_live[0] | (column == 1) & head_live[1])[:, None, None]
    own_panel = jnp.where(column == 0, first_rows, second_rows)
    head_blocks = jnp.where(keep_mask, own_panel, trailing[:slot_count])
    factored = jnp.concatenate([head_blocks, trailing[slot_count:]], axis=0)
    return factored[:, None]


def solution(mesh):
    row_count = mesh.shape["row"]
    col_count = mesh.shape["col"]
    devices = np.asarray(mesh.devices).reshape(
        row_count, col_count // row_count, row_count // X_SIZE, X_SIZE
    )
    split_mesh = Mesh(devices, ("row",) + COL_AXES)
    return jax.shard_map(
        per_device,
        mesh=split_mesh,
        in_specs=(
            P("row", COL_AXES, None, None),
            P(None, "row"),
            P(None, "row", COL_AXES),
            P(),
            P(),
        ),
        out_specs=P("row", COL_AXES, None, None),
        check_vma=False,
    )
```

```python
import jax
import jax.numpy as jnp
import numpy as np
from jax import lax
from jax.sharding import Mesh
from jax.sharding import PartitionSpec as P

PER_CLASS = 2
X_SIZE = 4


HIGHEST_PRECISION = lax.Precision.HIGHEST
PRODUCT_PRECISION = lax.Precision.HIGH
COL_AXES = ("zh", "zl", "x")
CLASS_AXES = ("zl", "x")


def apply_inverse(panel_rows_block, inverse):
    return jnp.einsum("ab,cb->ac", panel_rows_block, inverse, precision=HIGHEST_PRECISION)


def per_device(blocks, panel_rows, target_slots, diag_inverse, cross_block):
    row_count = lax.axis_size("row")
    col_count = lax.axis_size(COL_AXES)
    column = lax.axis_index(COL_AXES)
    stored = blocks[:, 0]
    slot_count = panel_rows.shape[1]
    block = stored.shape[-1]
    head_part = stored[:slot_count]
    chunk = slot_count * block // col_count
    pieces = head_part.reshape(col_count, chunk, block)
    received = lax.all_to_all(pieces, COL_AXES, 0, 0, tiled=True)
    zero_rows = received[0]
    one_rows = received[1]
    piece_slot = column * chunk // block
    first_live = lax.dynamic_index_in_dim(panel_rows[0], piece_slot, keepdims=False) >= 0
    second_live = lax.dynamic_index_in_dim(panel_rows[1], piece_slot, keepdims=False) >= 0
    cross_factor = jnp.dot(cross_block, diag_inverse[0].T, precision=HIGHEST_PRECISION)
    first_piece = jnp.where(first_live, apply_inverse(zero_rows, diag_inverse[0]), 0.0)
    updated_piece = one_rows - apply_inverse(first_piece, cross_factor)
    second_piece = jnp.where(second_live, apply_inverse(updated_piece, diag_inverse[1]), 0.0)
    both_pieces = jnp.stack([first_piece, second_piece])
    class_size = lax.axis_size(CLASS_AXES)
    swap = [(a * class_size + b, b * class_size + a) for a in range(row_count) for b in range(class_size)]
    swapped = lax.ppermute(both_pieces, ("row",) + CLASS_AXES, swap)
    spread = jnp.broadcast_to(swapped[None], (row_count,) + swapped.shape)
    class_pieces = lax.all_to_all(spread, "row", 0, 0, tiled=True)
    per_slot = block // chunk
    class_pieces = class_pieces.reshape(PER_CLASS, per_slot, 2, chunk, block)
    both_cols = class_pieces.transpose(2, 0, 1, 3, 4).reshape(2, PER_CLASS, block, block)
    both_rows = lax.all_gather(both_pieces, "x", axis=1, tiled=True)
    both_rows = lax.all_gather(both_rows, ("zh", "zl"), axis=1, tiled=True)
    both_rows = both_rows.reshape(2, slot_count, block, block)
    first_rows = both_rows[0]
    second_rows = both_rows[1]
    class_start = column // row_count * PER_CLASS
    row_index = target_slots[0, :, 0]
    col_index = target_slots[1, :, 0]
    present = row_index >= 0
    left_slot = jnp.where(present, row_index, 0)
    right_slot = jnp.where(present, col_index - class_start, 0)
    products = jnp.einsum("fakm,fbjm->akbj", both_rows, both_cols, precision=PRODUCT_PRECISION)
    schur_term = products[left_slot, :, right_slot, :]
    trailing = stored - jnp.where(present[:, None, None], schur_term, 0.0)
    head_live = panel_rows >= 0
    keep_mask = ((column == 0) & head_live[0] | (column == 1) & head_live[1])[:, None, None]
    own_panel = jnp.where(column == 0, first_rows, second_rows)
    head_blocks = jnp.where(keep_mask, own_panel, trailing[:slot_count])
    factored = jnp.concatenate([head_blocks, trailing[slot_count:]], axis=0)
    return factored[:, None]


def solution(mesh):
    row_count = mesh.shape["row"]
    col_count = mesh.shape["col"]
    devices = np.asarray(mesh.devices).reshape(
        row_count, col_count // row_count, row_count // X_SIZE, X_SIZE
    )
    split_mesh = Mesh(devices, ("row",) + COL_AXES)
    return jax.shard_map(
        per_device,
        mesh=split_mesh,
        in_specs=(
            P("row", COL_AXES, None, None),
            P(None, "row"),
            P(None, "row", COL_AXES),
            P(),
            P(),
        ),
        out_specs=P("row", COL_AXES, None, None),
        check_vma=False,
    )
```

```python
import jax
import jax.numpy as jnp
import numpy as np
from jax import lax
from jax.experimental import pallas as pl
from jax.experimental.pallas import tpu as pltpu
from jax.sharding import Mesh
from jax.sharding import PartitionSpec as P

PER_CLASS = 2
X_SIZE = 4


HIGHEST_PRECISION = lax.Precision.HIGHEST
PRODUCT_PRECISION = lax.Precision.HIGH
COL_AXES = ("zh", "zl", "x")
CLASS_AXES = ("zl", "x")


def apply_inverse(panel_rows_block, inverse):
    return jnp.einsum("ab,cb->ac", panel_rows_block, inverse, precision=HIGHEST_PRECISION)


def tail_kernel(table_ref, stored_ref, product_ref, panel_ref, out_ref):
    slot = pl.program_id(0)
    kept = stored_ref[...] - jnp.where(table_ref[2, slot] > 0, product_ref[...], 0.0)
    out_ref[...] = jnp.where(table_ref[3, slot] > 0, panel_ref[...], kept)


def finish_slots(table, stored, products, panels):
    slots, block, _ = stored.shape
    head = panels.shape[0] // 2
    spec = pltpu.PrefetchScalarGridSpec(
        num_scalar_prefetch=1,
        grid=(slots,),
        in_specs=[
            pl.BlockSpec((1, block, block), lambda s, t: (s, 0, 0)),
            pl.BlockSpec((1, block, block), lambda s, t: (t[0, s], 0, t[1, s])),
            pl.BlockSpec(
                (1, block, block), lambda s, t: (t[4, 0] * head + jnp.minimum(s, head - 1), 0, 0)
            ),
        ],
        out_specs=pl.BlockSpec((1, block, block), lambda s, t: (s, 0, 0)),
    )
    return pl.pallas_call(
        tail_kernel, grid_spec=spec, out_shape=jax.ShapeDtypeStruct(stored.shape, stored.dtype)
    )(table, stored, products, panels)


def per_device(blocks, panel_rows, target_slots, diag_inverse, cross_block):
    row_count = lax.axis_size("row")
    col_count = lax.axis_size(COL_AXES)
    column = lax.axis_index(COL_AXES)
    stored = blocks[:, 0]
    slot_count = panel_rows.shape[1]
    block = stored.shape[-1]
    head_part = stored[:slot_count]
    chunk = slot_count * block // col_count
    pieces = head_part.reshape(col_count, chunk, block)
    received = lax.all_to_all(pieces, COL_AXES, 0, 0, tiled=True)
    zero_rows = received[0]
    one_rows = received[1]
    piece_slot = column * chunk // block
    first_live = lax.dynamic_index_in_dim(panel_rows[0], piece_slot, keepdims=False) >= 0
    second_live = lax.dynamic_index_in_dim(panel_rows[1], piece_slot, keepdims=False) >= 0
    cross_factor = jnp.dot(cross_block, diag_inverse[0].T, precision=HIGHEST_PRECISION)
    first_piece = jnp.where(first_live, apply_inverse(zero_rows, diag_inverse[0]), 0.0)
    updated_piece = one_rows - apply_inverse(first_piece, cross_factor)
    second_piece = jnp.where(second_live, apply_inverse(updated_piece, diag_inverse[1]), 0.0)
    both_pieces = jnp.stack([first_piece, second_piece])
    class_size = lax.axis_size(CLASS_AXES)
    swap = [(a * class_size + b, b * class_size + a) for a in range(row_count) for b in range(class_size)]
    swapped = lax.ppermute(both_pieces, ("row",) + CLASS_AXES, swap)
    spread = jnp.broadcast_to(swapped[None], (row_count,) + swapped.shape)
    class_pieces = lax.all_to_all(spread, "row", 0, 0, tiled=True)
    per_slot = block // chunk
    class_pieces = class_pieces.reshape(PER_CLASS, per_slot, 2, chunk, block)
    both_cols = class_pieces.transpose(2, 0, 1, 3, 4).reshape(2, PER_CLASS, block, block)
    both_rows = lax.all_gather(both_pieces, "x", axis=1, tiled=True)
    both_rows = lax.all_gather(both_rows, ("zh", "zl"), axis=1, tiled=True)
    both_rows = both_rows.reshape(2, slot_count, block, block)
    class_start = column // row_count * PER_CLASS
    row_index = target_slots[0, :, 0]
    col_index = target_slots[1, :, 0]
    present = row_index >= 0
    left_slot = jnp.clip(jnp.where(present, row_index, 0), 0, slot_count - 1)
    right_slot = jnp.clip(jnp.where(present, col_index - class_start, 0), 0, PER_CLASS - 1)
    products = jnp.einsum("fakm,fbjm->akbj", both_rows, both_cols, precision=PRODUCT_PRECISION)
    products = products.reshape(slot_count, block, PER_CLASS * block)
    head_live = panel_rows >= 0
    keep_head = (column == 0) & head_live[0] | (column == 1) & head_live[1]
    slots = stored.shape[0]
    keep = jnp.zeros((slots,), jnp.bool_).at[:slot_count].set(keep_head)
    panel_column = jnp.full((slots,), column == 1)
    table = jnp.stack([left_slot, right_slot, present, keep, panel_column]).astype(jnp.int32)
    panels = both_rows.reshape(2 * slot_count, block, block)
    factored = finish_slots(table, stored, products, panels)
    return factored[:, None]


def solution(mesh):
    row_count = mesh.shape["row"]
    col_count = mesh.shape["col"]
    devices = np.asarray(mesh.devices).reshape(
        row_count, col_count // row_count, row_count // X_SIZE, X_SIZE
    )
    split_mesh = Mesh(devices, ("row",) + COL_AXES)
    return jax.shard_map(
        per_device,
        mesh=split_mesh,
        in_specs=(
            P("row", COL_AXES, None, None),
            P(None, "row"),
            P(None, "row", COL_AXES),
            P(),
            P(),
        ),
        out_specs=P("row", COL_AXES, None, None),
        check_vma=False,
    )
```

```python
import jax
import jax.numpy as jnp
import numpy as np
from jax import lax
from jax.experimental import pallas as pl
from jax.experimental.pallas import tpu as pltpu
from jax.sharding import Mesh
from jax.sharding import PartitionSpec as P

PER_CLASS = 2
X_SIZE = 4
HALVES = 2


HIGHEST_PRECISION = lax.Precision.HIGHEST
PRODUCT_PRECISION = lax.Precision.HIGH
COL_AXES = ("zh", "zl", "x")
CLASS_AXES = ("zl", "x")


def apply_inverse(panel_rows_block, inverse):
    return jnp.einsum("ab,cb->ac", panel_rows_block, inverse, precision=HIGHEST_PRECISION)


def tail_kernel(table_ref, stored_ref, product_ref, panel_ref, out_ref):
    slot = pl.program_id(0)
    kept = stored_ref[...] - jnp.where(table_ref[2, slot] > 0, product_ref[...], 0.0)
    out_ref[...] = jnp.where(table_ref[3, slot] > 0, panel_ref[...], kept)


def finish_slots(table, stored, products, panels):
    slots, block, _ = stored.shape
    head = panels.shape[0] // 2
    spec = pltpu.PrefetchScalarGridSpec(
        num_scalar_prefetch=1,
        grid=(slots,),
        in_specs=[
            pl.BlockSpec((1, block, block), lambda s, t: (s, 0, 0)),
            pl.BlockSpec((1, block, block), lambda s, t: (t[0, s], 0, t[1, s])),
            pl.BlockSpec(
                (1, block, block), lambda s, t: (t[4, 0] * head + jnp.minimum(s, head - 1), 0, 0)
            ),
        ],
        out_specs=pl.BlockSpec((1, block, block), lambda s, t: (s, 0, 0)),
    )
    return pl.pallas_call(
        tail_kernel, grid_spec=spec, out_shape=jax.ShapeDtypeStruct(stored.shape, stored.dtype)
    )(table, stored, products, panels)


def per_device(blocks, panel_rows, target_slots, diag_inverse, cross_block):
    row_count = lax.axis_size("row")
    col_count = lax.axis_size(COL_AXES)
    column = lax.axis_index(COL_AXES)
    stored = blocks[:, 0]
    slot_count = panel_rows.shape[1]
    block = stored.shape[-1]
    head_part = stored[:slot_count]
    chunk = slot_count * block // col_count
    pieces = head_part.reshape(col_count, chunk, block)
    piece_slot = column * chunk // block
    first_live = lax.dynamic_index_in_dim(panel_rows[0], piece_slot, keepdims=False) >= 0
    second_live = lax.dynamic_index_in_dim(panel_rows[1], piece_slot, keepdims=False) >= 0
    cross_factor = jnp.dot(cross_block, diag_inverse[0].T, precision=HIGHEST_PRECISION)
    class_size = lax.axis_size(CLASS_AXES)
    swap = [(a * class_size + b, b * class_size + a) for a in range(row_count) for b in range(class_size)]
    half = chunk // HALVES
    row_parts = []
    col_parts = []
    for part in range(HALVES):
        received = lax.all_to_all(pieces[:, part * half:(part + 1) * half], COL_AXES, 0, 0, tiled=True)
        zero_rows = received[0]
        one_rows = received[1]
        first_piece = jnp.where(first_live, apply_inverse(zero_rows, diag_inverse[0]), 0.0)
        updated_piece = one_rows - apply_inverse(first_piece, cross_factor)
        second_piece = jnp.where(second_live, apply_inverse(updated_piece, diag_inverse[1]), 0.0)
        both_pieces = jnp.stack([first_piece, second_piece])
        swapped = lax.ppermute(both_pieces, ("row",) + CLASS_AXES, swap)
        spread = jnp.broadcast_to(swapped[None], (row_count,) + swapped.shape)
        col_parts.append(lax.all_to_all(spread, "row", 0, 0, tiled=True))
        gathered = lax.all_gather(both_pieces, "x", axis=1, tiled=True)
        row_parts.append(lax.all_gather(gathered, ("zh", "zl"), axis=1, tiled=True))
    per_slot = block // chunk
    both_rows = jnp.stack(
        [part.reshape(2, slot_count, per_slot, half, block) for part in row_parts], axis=3
    ).reshape(2, slot_count, block, block)
    class_pieces = jnp.stack(col_parts, axis=2).reshape(PER_CLASS, per_slot, 2, chunk, block)
    both_cols = class_pieces.transpose(2, 0, 1, 3, 4).reshape(2, PER_CLASS, block, block)
    class_start = column // row_count * PER_CLASS
    row_index = target_slots[0, :, 0]
    col_index = target_slots[1, :, 0]
    present = row_index >= 0
    left_slot = jnp.clip(jnp.where(present, row_index, 0), 0, slot_count - 1)
    right_slot = jnp.clip(jnp.where(present, col_index - class_start, 0), 0, PER_CLASS - 1)
    products = jnp.einsum("fakm,fbjm->akbj", both_rows, both_cols, precision=PRODUCT_PRECISION)
    products = products.reshape(slot_count, block, PER_CLASS * block)
    head_live = panel_rows >= 0
    keep_head = (column == 0) & head_live[0] | (column == 1) & head_live[1]
    slots = stored.shape[0]
    keep = jnp.zeros((slots,), jnp.bool_).at[:slot_count].set(keep_head)
    panel_column = jnp.full((slots,), column == 1)
    table = jnp.stack([left_slot, right_slot, present, keep, panel_column]).astype(jnp.int32)
    panels = both_rows.reshape(2 * slot_count, block, block)
    factored = finish_slots(table, stored, products, panels)
    return factored[:, None]


def solution(mesh):
    row_count = mesh.shape["row"]
    col_count = mesh.shape["col"]
    devices = np.asarray(mesh.devices).reshape(
        row_count, col_count // row_count, row_count // X_SIZE, X_SIZE
    )
    split_mesh = Mesh(devices, ("row",) + COL_AXES)
    return jax.shard_map(
        per_device,
        mesh=split_mesh,
        in_specs=(
            P("row", COL_AXES, None, None),
            P(None, "row"),
            P(None, "row", COL_AXES),
            P(),
            P(),
        ),
        out_specs=P("row", COL_AXES, None, None),
        check_vma=False,
    )
```

```python
import jax
import jax.numpy as jnp
import numpy as np
from jax import lax
from jax.experimental import pallas as pl
from jax.experimental.pallas import tpu as pltpu
from jax.sharding import Mesh
from jax.sharding import PartitionSpec as P

PER_CLASS = 2
X_SIZE = 4


HIGHEST_PRECISION = lax.Precision.HIGHEST
TRANSPOSED_RIGHT = (((1,), (1,)), ((), ()))
COL_AXES = ("zh", "zl", "x")
CLASS_AXES = ("zl", "x")


def apply_inverse(panel_rows_block, inverse):
    return jnp.einsum("ab,cb->ac", panel_rows_block, inverse, precision=HIGHEST_PRECISION)


def tail_kernel(table_ref, stored_ref, left_one, left_two, right_one, right_two, panel_ref, out_ref):
    slot = pl.program_id(0)
    schur = lax.dot_general(
        left_one[0], right_one[0], TRANSPOSED_RIGHT, precision=HIGHEST_PRECISION,
        preferred_element_type=jnp.float32,
    )
    schur += lax.dot_general(
        left_two[0], right_two[0], TRANSPOSED_RIGHT, precision=HIGHEST_PRECISION,
        preferred_element_type=jnp.float32,
    )
    kept = stored_ref[0] - jnp.where(table_ref[2, slot] > 0, schur, 0.0)
    out_ref[0] = jnp.where(table_ref[3, slot] > 0, panel_ref[0], kept)


def finish_slots(table, stored, rows, cols):
    slots, block, _ = stored.shape
    head = rows.shape[0] // 2
    classes = cols.shape[0] // 2
    tile = (1, block, block)
    spec = pltpu.PrefetchScalarGridSpec(
        num_scalar_prefetch=1,
        grid=(slots,),
        in_specs=[
            pl.BlockSpec(tile, lambda s, t: (s, 0, 0)),
            pl.BlockSpec(tile, lambda s, t: (t[0, s], 0, 0)),
            pl.BlockSpec(tile, lambda s, t: (head + t[0, s], 0, 0)),
            pl.BlockSpec(tile, lambda s, t: (t[1, s], 0, 0)),
            pl.BlockSpec(tile, lambda s, t: (classes + t[1, s], 0, 0)),
            pl.BlockSpec(tile, lambda s, t: (t[4, 0] * head + jnp.minimum(s, head - 1), 0, 0)),
        ],
        out_specs=pl.BlockSpec(tile, lambda s, t: (s, 0, 0)),
    )
    return pl.pallas_call(
        tail_kernel, grid_spec=spec, out_shape=jax.ShapeDtypeStruct(stored.shape, stored.dtype)
    )(table, stored, rows, rows, cols, cols, rows)


def per_device(blocks, panel_rows, target_slots, diag_inverse, cross_block):
    row_count = lax.axis_size("row")
    col_count = lax.axis_size(COL_AXES)
    column = lax.axis_index(COL_AXES)
    stored = blocks[:, 0]
    slot_count = panel_rows.shape[1]
    block = stored.shape[-1]
    head_part = stored[:slot_count]
    chunk = slot_count * block // col_count
    pieces = head_part.reshape(col_count, chunk, block)
    received = lax.all_to_all(pieces, COL_AXES, 0, 0, tiled=True)
    zero_rows = received[0]
    one_rows = received[1]
    piece_slot = column * chunk // block
    first_live = lax.dynamic_index_in_dim(panel_rows[0], piece_slot, keepdims=False) >= 0
    second_live = lax.dynamic_index_in_dim(panel_rows[1], piece_slot, keepdims=False) >= 0
    cross_factor = jnp.dot(cross_block, diag_inverse[0].T, precision=HIGHEST_PRECISION)
    first_piece = jnp.where(first_live, apply_inverse(zero_rows, diag_inverse[0]), 0.0)
    updated_piece = one_rows - apply_inverse(first_piece, cross_factor)
    second_piece = jnp.where(second_live, apply_inverse(updated_piece, diag_inverse[1]), 0.0)
    both_pieces = jnp.stack([first_piece, second_piece])
    class_size = lax.axis_size(CLASS_AXES)
    swap = [(a * class_size + b, b * class_size + a) for a in range(row_count) for b in range(class_size)]
    swapped = lax.ppermute(both_pieces, ("row",) + CLASS_AXES, swap)
    spread = jnp.broadcast_to(swapped[None], (row_count,) + swapped.shape)
    class_pieces = lax.all_to_all(spread, "row", 0, 0, tiled=True)
    per_slot = block // chunk
    class_pieces = class_pieces.reshape(PER_CLASS, per_slot, 2, chunk, block)
    both_cols = class_pieces.transpose(2, 0, 1, 3, 4).reshape(2, PER_CLASS, block, block)
    both_rows = lax.all_gather(both_pieces, "x", axis=1, tiled=True)
    both_rows = lax.all_gather(both_rows, ("zh", "zl"), axis=1, tiled=True)
    both_rows = both_rows.reshape(2, slot_count, block, block)
    class_start = column // row_count * PER_CLASS
    row_index = target_slots[0, :, 0]
    col_index = target_slots[1, :, 0]
    present = row_index >= 0
    left_slot = jnp.clip(jnp.where(present, row_index, 0), 0, slot_count - 1)
    right_slot = jnp.clip(jnp.where(present, col_index - class_start, 0), 0, PER_CLASS - 1)
    head_live = panel_rows >= 0
    keep_head = (column == 0) & head_live[0] | (column == 1) & head_live[1]
    slots = stored.shape[0]
    keep = jnp.zeros((slots,), jnp.bool_).at[:slot_count].set(keep_head)
    panel_column = jnp.full((slots,), column == 1)
    table = jnp.stack([left_slot, right_slot, present, keep, panel_column]).astype(jnp.int32)
    rows = both_rows.reshape(2 * slot_count, block, block)
    cols = both_cols.reshape(2 * PER_CLASS, block, block)
    factored = finish_slots(table, stored, rows, cols)
    return factored[:, None]


def solution(mesh):
    row_count = mesh.shape["row"]
    col_count = mesh.shape["col"]
    devices = np.asarray(mesh.devices).reshape(
        row_count, col_count // row_count, row_count // X_SIZE, X_SIZE
    )
    split_mesh = Mesh(devices, ("row",) + COL_AXES)
    return jax.shard_map(
        per_device,
        mesh=split_mesh,
        in_specs=(
            P("row", COL_AXES, None, None),
            P(None, "row"),
            P(None, "row", COL_AXES),
            P(),
            P(),
        ),
        out_specs=P("row", COL_AXES, None, None),
        check_vma=False,
    )
```

```python
import jax
import jax.numpy as jnp
import numpy as np
from jax import lax
from jax.experimental import pallas as pl
from jax.experimental.pallas import tpu as pltpu
from jax.sharding import Mesh
from jax.sharding import PartitionSpec as P

PER_CLASS = 2
X_SIZE = 4


HIGHEST_PRECISION = lax.Precision.HIGHEST
PRODUCT_PRECISION = lax.Precision.HIGH
TRANSPOSED_RIGHT = (((1,), (1,)), ((), ()))
COL_AXES = ("zh", "zl", "x")
CLASS_AXES = ("zl", "x")


def apply_inverse(panel_rows_block, inverse):
    return jnp.einsum("ab,cb->ac", panel_rows_block, inverse, precision=HIGHEST_PRECISION)


def tail_kernel(table_ref, stored_ref, left_one, left_two, right_one, right_two, panel_ref, out_ref):
    slot = pl.program_id(0)
    schur = lax.dot_general(
        left_one[0], right_one[0], TRANSPOSED_RIGHT, precision=PRODUCT_PRECISION,
        preferred_element_type=jnp.float32,
    )
    schur += lax.dot_general(
        left_two[0], right_two[0], TRANSPOSED_RIGHT, precision=PRODUCT_PRECISION,
        preferred_element_type=jnp.float32,
    )
    kept = stored_ref[0] - jnp.where(table_ref[2, slot] > 0, schur, 0.0)
    out_ref[0] = jnp.where(table_ref[3, slot] > 0, panel_ref[0], kept)


def finish_slots(table, stored, rows, cols):
    slots, block, _ = stored.shape
    head = rows.shape[0] // 2
    classes = cols.shape[0] // 2
    tile = (1, block, block)
    spec = pltpu.PrefetchScalarGridSpec(
        num_scalar_prefetch=1,
        grid=(slots,),
        in_specs=[
            pl.BlockSpec(tile, lambda s, t: (s, 0, 0)),
            pl.BlockSpec(tile, lambda s, t: (t[0, s], 0, 0)),
            pl.BlockSpec(tile, lambda s, t: (head + t[0, s], 0, 0)),
            pl.BlockSpec(tile, lambda s, t: (t[1, s], 0, 0)),
            pl.BlockSpec(tile, lambda s, t: (classes + t[1, s], 0, 0)),
            pl.BlockSpec(tile, lambda s, t: (t[4, 0] * head + jnp.minimum(s, head - 1), 0, 0)),
        ],
        out_specs=pl.BlockSpec(tile, lambda s, t: (s, 0, 0)),
    )
    return pl.pallas_call(
        tail_kernel, grid_spec=spec, out_shape=jax.ShapeDtypeStruct(stored.shape, stored.dtype)
    )(table, stored, rows, rows, cols, cols, rows)


def per_device(blocks, panel_rows, target_slots, diag_inverse, cross_block):
    row_count = lax.axis_size("row")
    col_count = lax.axis_size(COL_AXES)
    column = lax.axis_index(COL_AXES)
    stored = blocks[:, 0]
    slot_count = panel_rows.shape[1]
    block = stored.shape[-1]
    head_part = stored[:slot_count]
    chunk = slot_count * block // col_count
    pieces = head_part.reshape(col_count, chunk, block)
    received = lax.all_to_all(pieces, COL_AXES, 0, 0, tiled=True)
    zero_rows = received[0]
    one_rows = received[1]
    piece_slot = column * chunk // block
    first_live = lax.dynamic_index_in_dim(panel_rows[0], piece_slot, keepdims=False) >= 0
    second_live = lax.dynamic_index_in_dim(panel_rows[1], piece_slot, keepdims=False) >= 0
    cross_factor = jnp.dot(cross_block, diag_inverse[0].T, precision=HIGHEST_PRECISION)
    first_piece = jnp.where(first_live, apply_inverse(zero_rows, diag_inverse[0]), 0.0)
    updated_piece = one_rows - apply_inverse(first_piece, cross_factor)
    second_piece = jnp.where(second_live, apply_inverse(updated_piece, diag_inverse[1]), 0.0)
    both_pieces = jnp.stack([first_piece, second_piece])
    class_size = lax.axis_size(CLASS_AXES)
    swap = [(a * class_size + b, b * class_size + a) for a in range(row_count) for b in range(class_size)]
    swapped = lax.ppermute(both_pieces, ("row",) + CLASS_AXES, swap)
    spread = jnp.broadcast_to(swapped[None], (row_count,) + swapped.shape)
    class_pieces = lax.all_to_all(spread, "row", 0, 0, tiled=True)
    per_slot = block // chunk
    class_pieces = class_pieces.reshape(PER_CLASS, per_slot, 2, chunk, block)
    both_cols = class_pieces.transpose(2, 0, 1, 3, 4).reshape(2, PER_CLASS, block, block)
    both_rows = lax.all_gather(both_pieces, "x", axis=1, tiled=True)
    both_rows = lax.all_gather(both_rows, ("zh", "zl"), axis=1, tiled=True)
    both_rows = both_rows.reshape(2, slot_count, block, block)
    class_start = column // row_count * PER_CLASS
    row_index = target_slots[0, :, 0]
    col_index = target_slots[1, :, 0]
    present = row_index >= 0
    left_slot = jnp.clip(jnp.where(present, row_index, 0), 0, slot_count - 1)
    right_slot = jnp.clip(jnp.where(present, col_index - class_start, 0), 0, PER_CLASS - 1)
    head_live = panel_rows >= 0
    keep_head = (column == 0) & head_live[0] | (column == 1) & head_live[1]
    slots = stored.shape[0]
    keep = jnp.zeros((slots,), jnp.bool_).at[:slot_count].set(keep_head)
    panel_column = jnp.full((slots,), column == 1)
    table = jnp.stack([left_slot, right_slot, present, keep, panel_column]).astype(jnp.int32)
    rows = both_rows.reshape(2 * slot_count, block, block)
    cols = both_cols.reshape(2 * PER_CLASS, block, block)
    factored = finish_slots(table, stored, rows, cols)
    return factored[:, None]


def solution(mesh):
    row_count = mesh.shape["row"]
    col_count = mesh.shape["col"]
    devices = np.asarray(mesh.devices).reshape(
        row_count, col_count // row_count, row_count // X_SIZE, X_SIZE
    )
    split_mesh = Mesh(devices, ("row",) + COL_AXES)
    return jax.shard_map(
        per_device,
        mesh=split_mesh,
        in_specs=(
            P("row", COL_AXES, None, None),
            P(None, "row"),
            P(None, "row", COL_AXES),
            P(),
            P(),
        ),
        out_specs=P("row", COL_AXES, None, None),
        check_vma=False,
    )
```

```python
import jax
import jax.numpy as jnp
import numpy as np
from jax import lax
from jax.experimental import pallas as pl
from jax.experimental.pallas import tpu as pltpu
from jax.sharding import Mesh
from jax.sharding import PartitionSpec as P

PER_CLASS = 2
X_SIZE = 4


HIGHEST_PRECISION = lax.Precision.HIGHEST
PRODUCT_PRECISION = lax.Precision.HIGH
TRANSPOSED_RIGHT = (((1,), (1,)), ((), ()))
COL_AXES = ("zh", "zl", "x")
CLASS_AXES = ("zl", "x")
Z_AXES = ("zh", "zl")


def apply_inverse(panel_rows_block, inverse):
    return jnp.einsum("ab,cb->ac", panel_rows_block, inverse, precision=HIGHEST_PRECISION)


def tail_kernel(table_ref, stored_ref, left_one, left_two, right_one, right_two, panel_ref, out_ref):
    slot = pl.program_id(0)
    schur = lax.dot_general(
        left_one[0], right_one[0], TRANSPOSED_RIGHT, precision=PRODUCT_PRECISION,
        preferred_element_type=jnp.float32,
    )
    schur += lax.dot_general(
        left_two[0], right_two[0], TRANSPOSED_RIGHT, precision=PRODUCT_PRECISION,
        preferred_element_type=jnp.float32,
    )
    kept = stored_ref[0] - jnp.where(table_ref[2, slot] > 0, schur, 0.0)
    out_ref[0] = jnp.where(table_ref[3, slot] > 0, panel_ref[0], kept)


def finish_slots(table, stored, rows, cols):
    slots, block, _ = stored.shape
    head = rows.shape[0] // 2
    classes = cols.shape[0] // 2
    tile = (1, block, block)
    spec = pltpu.PrefetchScalarGridSpec(
        num_scalar_prefetch=1,
        grid=(slots,),
        in_specs=[
            pl.BlockSpec(tile, lambda s, t: (s, 0, 0)),
            pl.BlockSpec(tile, lambda s, t: (t[0, s], 0, 0)),
            pl.BlockSpec(tile, lambda s, t: (head + t[0, s], 0, 0)),
            pl.BlockSpec(tile, lambda s, t: (t[1, s], 0, 0)),
            pl.BlockSpec(tile, lambda s, t: (classes + t[1, s], 0, 0)),
            pl.BlockSpec(
                tile, lambda s, t: (t[4, 0] * head + (jnp.minimum(s, head - 1) - t[5, 0] + head) % head, 0, 0)
            ),
        ],
        out_specs=pl.BlockSpec(tile, lambda s, t: (s, 0, 0)),
    )
    return pl.pallas_call(
        tail_kernel, grid_spec=spec, out_shape=jax.ShapeDtypeStruct(stored.shape, stored.dtype)
    )(table, stored, rows, rows, cols, cols, rows)


def per_device(blocks, panel_rows, target_slots, diag_inverse, cross_block):
    row_count = lax.axis_size("row")
    col_count = lax.axis_size(COL_AXES)
    column = lax.axis_index(COL_AXES)
    stored = blocks[:, 0]
    slot_count = panel_rows.shape[1]
    block = stored.shape[-1]
    head_part = stored[:slot_count]
    chunk = slot_count * block // col_count
    pieces = head_part.reshape(col_count, chunk, block)
    received = lax.all_to_all(pieces, COL_AXES, 0, 0, tiled=True)
    zero_rows = received[0]
    one_rows = received[1]
    piece_slot = column * chunk // block
    first_live = lax.dynamic_index_in_dim(panel_rows[0], piece_slot, keepdims=False) >= 0
    second_live = lax.dynamic_index_in_dim(panel_rows[1], piece_slot, keepdims=False) >= 0
    cross_factor = jnp.dot(cross_block, diag_inverse[0].T, precision=HIGHEST_PRECISION)
    first_piece = jnp.where(first_live, apply_inverse(zero_rows, diag_inverse[0]), 0.0)
    updated_piece = one_rows - apply_inverse(first_piece, cross_factor)
    second_piece = jnp.where(second_live, apply_inverse(updated_piece, diag_inverse[1]), 0.0)
    both_pieces = jnp.stack([first_piece, second_piece])
    class_size = lax.axis_size(CLASS_AXES)
    swap = [(a * class_size + b, b * class_size + a) for a in range(row_count) for b in range(class_size)]
    swapped = lax.ppermute(both_pieces, ("row",) + CLASS_AXES, swap)
    spread = jnp.broadcast_to(swapped[None], (row_count,) + swapped.shape)
    class_pieces = lax.all_to_all(spread, "row", 0, 0, tiled=True)
    per_slot = block // chunk
    class_pieces = class_pieces.reshape(PER_CLASS, per_slot, 2, chunk, block)
    both_cols = class_pieces.transpose(2, 0, 1, 3, 4).reshape(2, PER_CLASS, block, block)
    own_slot = lax.all_gather(both_pieces, "x", axis=1, tiled=True)
    ring = lax.axis_size(Z_AXES)
    ring_place = lax.axis_index(Z_AXES)
    forward = [(i, (i + 1) % ring) for i in range(ring)]
    backward = [(i, (i - 1) % ring) for i in range(ring)]
    by_offset = [own_slot] * ring
    ahead = own_slot
    behind = own_slot
    for step in range(1, ring // 2 + 1):
        ahead = lax.ppermute(ahead, Z_AXES, forward)
        by_offset[ring - step] = ahead
        if step < ring - step:
            behind = lax.ppermute(behind, Z_AXES, backward)
            by_offset[step] = behind
    rows_by_offset = jnp.stack(by_offset, axis=1)
    class_start = column // row_count * PER_CLASS
    row_index = target_slots[0, :, 0]
    col_index = target_slots[1, :, 0]
    present = row_index >= 0
    left_slot = jnp.clip(jnp.where(present, row_index, 0), 0, slot_count - 1)
    left_slot = (left_slot - ring_place) % ring
    right_slot = jnp.clip(jnp.where(present, col_index - class_start, 0), 0, PER_CLASS - 1)
    head_live = panel_rows >= 0
    keep_head = (column == 0) & head_live[0] | (column == 1) & head_live[1]
    slots = stored.shape[0]
    keep = jnp.zeros((slots,), jnp.bool_).at[:slot_count].set(keep_head)
    panel_column = jnp.full((slots,), column == 1)
    place = jnp.full((slots,), ring_place)
    table = jnp.stack([left_slot, right_slot, present, keep, panel_column, place]).astype(jnp.int32)
    rows = rows_by_offset.reshape(2 * slot_count, block, block)
    cols = both_cols.reshape(2 * PER_CLASS, block, block)
    factored = finish_slots(table, stored, rows, cols)
    return factored[:, None]


def solution(mesh):
    row_count = mesh.shape["row"]
    col_count = mesh.shape["col"]
    devices = np.asarray(mesh.devices).reshape(
        row_count, col_count // row_count, row_count // X_SIZE, X_SIZE
    )
    split_mesh = Mesh(devices, ("row",) + COL_AXES)
    return jax.shard_map(
        per_device,
        mesh=split_mesh,
        in_specs=(
            P("row", COL_AXES, None, None),
            P(None, "row"),
            P(None, "row", COL_AXES),
            P(),
            P(),
        ),
        out_specs=P("row", COL_AXES, None, None),
        check_vma=False,
    )
```

```python
import jax
import jax.numpy as jnp
import numpy as np
from jax import lax
from jax.experimental import pallas as pl
from jax.experimental.pallas import tpu as pltpu
from jax.sharding import Mesh
from jax.sharding import PartitionSpec as P

PER_CLASS = 2
X_SIZE = 4


HIGHEST_PRECISION = lax.Precision.HIGHEST
PRODUCT_PRECISION = lax.Precision.HIGH
PLAIN_PRODUCT = (((1,), (0,)), ((), ()))
COL_AXES = ("zh", "zl", "x")
CLASS_AXES = ("zl", "x")


def apply_inverse(panel_rows_block, inverse):
    return jnp.einsum("ab,cb->ac", panel_rows_block, inverse, precision=HIGHEST_PRECISION)


def tail_kernel(table_ref, stored_ref, left_one, left_two, right_one, right_two, panel_ref, out_ref):
    slot = pl.program_id(0)
    schur = lax.dot_general(
        left_one[0], right_one[0], PLAIN_PRODUCT, precision=PRODUCT_PRECISION,
        preferred_element_type=jnp.float32,
    )
    schur += lax.dot_general(
        left_two[0], right_two[0], PLAIN_PRODUCT, precision=PRODUCT_PRECISION,
        preferred_element_type=jnp.float32,
    )
    kept = stored_ref[0] - jnp.where(table_ref[2, slot] > 0, schur, 0.0)
    out_ref[0] = jnp.where(table_ref[3, slot] > 0, panel_ref[0], kept)


def finish_slots(table, stored, rows, cols):
    slots, block, _ = stored.shape
    head = rows.shape[0] // 2
    classes = cols.shape[0] // 2
    tile = (1, block, block)
    spec = pltpu.PrefetchScalarGridSpec(
        num_scalar_prefetch=1,
        grid=(slots,),
        in_specs=[
            pl.BlockSpec(tile, lambda s, t: (s, 0, 0)),
            pl.BlockSpec(tile, lambda s, t: (t[0, s], 0, 0)),
            pl.BlockSpec(tile, lambda s, t: (head + t[0, s], 0, 0)),
            pl.BlockSpec(tile, lambda s, t: (t[1, s], 0, 0)),
            pl.BlockSpec(tile, lambda s, t: (classes + t[1, s], 0, 0)),
            pl.BlockSpec(tile, lambda s, t: (t[4, 0] * head + jnp.minimum(s, head - 1), 0, 0)),
        ],
        out_specs=pl.BlockSpec(tile, lambda s, t: (s, 0, 0)),
    )
    return pl.pallas_call(
        tail_kernel, grid_spec=spec, out_shape=jax.ShapeDtypeStruct(stored.shape, stored.dtype)
    )(table, stored, rows, rows, cols, cols, rows)


def per_device(blocks, panel_rows, target_slots, diag_inverse, cross_block):
    row_count = lax.axis_size("row")
    col_count = lax.axis_size(COL_AXES)
    column = lax.axis_index(COL_AXES)
    stored = blocks[:, 0]
    slot_count = panel_rows.shape[1]
    block = stored.shape[-1]
    head_part = stored[:slot_count]
    chunk = slot_count * block // col_count
    pieces = head_part.reshape(col_count, chunk, block)
    received = lax.all_to_all(pieces, COL_AXES, 0, 0, tiled=True)
    zero_rows = received[0]
    one_rows = received[1]
    piece_slot = column * chunk // block
    first_live = lax.dynamic_index_in_dim(panel_rows[0], piece_slot, keepdims=False) >= 0
    second_live = lax.dynamic_index_in_dim(panel_rows[1], piece_slot, keepdims=False) >= 0
    cross_factor = jnp.dot(cross_block, diag_inverse[0].T, precision=HIGHEST_PRECISION)
    first_piece = jnp.where(first_live, apply_inverse(zero_rows, diag_inverse[0]), 0.0)
    updated_piece = one_rows - apply_inverse(first_piece, cross_factor)
    second_piece = jnp.where(second_live, apply_inverse(updated_piece, diag_inverse[1]), 0.0)
    both_pieces = jnp.stack([first_piece, second_piece])
    class_size = lax.axis_size(CLASS_AXES)
    swap = [(a * class_size + b, b * class_size + a) for a in range(row_count) for b in range(class_size)]
    swapped = lax.ppermute(both_pieces, ("row",) + CLASS_AXES, swap)
    spread = jnp.broadcast_to(swapped[None], (row_count,) + swapped.shape)
    class_pieces = lax.all_to_all(spread, "row", 0, 0, tiled=True)
    per_slot = block // chunk
    class_pieces = class_pieces.reshape(PER_CLASS, per_slot, 2, chunk, block)
    both_cols = class_pieces.transpose(2, 0, 1, 3, 4).reshape(2, PER_CLASS, block, block)
    both_rows = lax.all_gather(both_pieces, "x", axis=1, tiled=True)
    both_rows = lax.all_gather(both_rows, ("zh", "zl"), axis=1, tiled=True)
    both_rows = both_rows.reshape(2, slot_count, block, block)
    class_start = column // row_count * PER_CLASS
    row_index = target_slots[0, :, 0]
    col_index = target_slots[1, :, 0]
    present = row_index >= 0
    left_slot = jnp.clip(jnp.where(present, row_index, 0), 0, slot_count - 1)
    right_slot = jnp.clip(jnp.where(present, col_index - class_start, 0), 0, PER_CLASS - 1)
    head_live = panel_rows >= 0
    keep_head = (column == 0) & head_live[0] | (column == 1) & head_live[1]
    slots = stored.shape[0]
    keep = jnp.zeros((slots,), jnp.bool_).at[:slot_count].set(keep_head)
    panel_column = jnp.full((slots,), column == 1)
    table = jnp.stack([left_slot, right_slot, present, keep, panel_column]).astype(jnp.int32)
    rows = both_rows.reshape(2 * slot_count, block, block)
    cols = jnp.swapaxes(both_cols.reshape(2 * PER_CLASS, block, block), 1, 2)
    factored = finish_slots(table, stored, rows, cols)
    return factored[:, None]


def solution(mesh):
    row_count = mesh.shape["row"]
    col_count = mesh.shape["col"]
    devices = np.asarray(mesh.devices).reshape(
        row_count, col_count // row_count, row_count // X_SIZE, X_SIZE
    )
    split_mesh = Mesh(devices, ("row",) + COL_AXES)
    return jax.shard_map(
        per_device,
        mesh=split_mesh,
        in_specs=(
            P("row", COL_AXES, None, None),
            P(None, "row"),
            P(None, "row", COL_AXES),
            P(),
            P(),
        ),
        out_specs=P("row", COL_AXES, None, None),
        check_vma=False,
    )
```

```python
import jax
import jax.numpy as jnp
import numpy as np
from jax import lax
from jax.experimental import pallas as pl
from jax.experimental.pallas import tpu as pltpu
from jax.sharding import Mesh
from jax.sharding import PartitionSpec as P

PER_CLASS = 2
X_SIZE = 4
SLOTS_PER_STEP = 2


HIGHEST_PRECISION = lax.Precision.HIGHEST
PRODUCT_PRECISION = lax.Precision.HIGH
PLAIN_PRODUCT = (((1,), (0,)), ((), ()))
COL_AXES = ("zh", "zl", "x")
CLASS_AXES = ("zl", "x")


def apply_inverse(panel_rows_block, inverse):
    return jnp.einsum("ab,cb->ac", panel_rows_block, inverse, precision=HIGHEST_PRECISION)


def tail_kernel(table_ref, stored_ref, *refs):
    lefts, rights, panels, out_ref = refs[:4], refs[4:8], refs[8:10], refs[10]
    step = pl.program_id(0)
    for j in range(SLOTS_PER_STEP):
        slot = step * SLOTS_PER_STEP + j
        schur = lax.dot_general(
            lefts[2 * j][0], rights[2 * j][0], PLAIN_PRODUCT, precision=PRODUCT_PRECISION,
            preferred_element_type=jnp.float32,
        )
        schur += lax.dot_general(
            lefts[2 * j + 1][0], rights[2 * j + 1][0], PLAIN_PRODUCT, precision=PRODUCT_PRECISION,
            preferred_element_type=jnp.float32,
        )
        kept = stored_ref[j] - jnp.where(table_ref[2, slot] > 0, schur, 0.0)
        out_ref[j] = jnp.where(table_ref[3, slot] > 0, panels[j][0], kept)


def finish_slots(table, stored, rows, cols):
    slots, block, _ = stored.shape
    head = rows.shape[0] // 2
    classes = cols.shape[0] // 2
    tile = (1, block, block)
    pair = (SLOTS_PER_STEP, block, block)
    left_specs = []
    right_specs = []
    panel_specs = []
    for j in range(SLOTS_PER_STEP):
        for f in range(2):
            left_specs.append(
                pl.BlockSpec(tile, lambda s, t, j=j, f=f: (f * head + t[0, s * SLOTS_PER_STEP + j], 0, 0))
            )
            right_specs.append(
                pl.BlockSpec(tile, lambda s, t, j=j, f=f: (f * classes + t[1, s * SLOTS_PER_STEP + j], 0, 0))
            )
        panel_specs.append(
            pl.BlockSpec(
                tile,
                lambda s, t, j=j: (t[4, 0] * head + jnp.minimum(s * SLOTS_PER_STEP + j, head - 1), 0, 0),
            )
        )
    spec = pltpu.PrefetchScalarGridSpec(
        num_scalar_prefetch=1,
        grid=(slots // SLOTS_PER_STEP,),
        in_specs=[pl.BlockSpec(pair, lambda s, t: (s, 0, 0))] + left_specs + right_specs + panel_specs,
        out_specs=pl.BlockSpec(pair, lambda s, t: (s, 0, 0)),
    )
    operands = [rows] * (2 * SLOTS_PER_STEP) + [cols] * (2 * SLOTS_PER_STEP) + [rows] * SLOTS_PER_STEP
    return pl.pallas_call(
        tail_kernel, grid_spec=spec, out_shape=jax.ShapeDtypeStruct(stored.shape, stored.dtype)
    )(table, stored, *operands)


def per_device(blocks, panel_rows, target_slots, diag_inverse, cross_block):
    row_count = lax.axis_size("row")
    col_count = lax.axis_size(COL_AXES)
    column = lax.axis_index(COL_AXES)
    stored = blocks[:, 0]
    slot_count = panel_rows.shape[1]
    block = stored.shape[-1]
    head_part = stored[:slot_count]
    chunk = slot_count * block // col_count
    pieces = head_part.reshape(col_count, chunk, block)
    received = lax.all_to_all(pieces, COL_AXES, 0, 0, tiled=True)
    zero_rows = received[0]
    one_rows = received[1]
    piece_slot = column * chunk // block
    first_live = lax.dynamic_index_in_dim(panel_rows[0], piece_slot, keepdims=False) >= 0
    second_live = lax.dynamic_index_in_dim(panel_rows[1], piece_slot, keepdims=False) >= 0
    cross_factor = jnp.dot(cross_block, diag_inverse[0].T, precision=HIGHEST_PRECISION)
    first_piece = jnp.where(first_live, apply_inverse(zero_rows, diag_inverse[0]), 0.0)
    updated_piece = one_rows - apply_inverse(first_piece, cross_factor)
    second_piece = jnp.where(second_live, apply_inverse(updated_piece, diag_inverse[1]), 0.0)
    both_pieces = jnp.stack([first_piece, second_piece])
    class_size = lax.axis_size(CLASS_AXES)
    swap = [(a * class_size + b, b * class_size + a) for a in range(row_count) for b in range(class_size)]
    swapped = lax.ppermute(both_pieces, ("row",) + CLASS_AXES, swap)
    spread = jnp.broadcast_to(swapped[None], (row_count,) + swapped.shape)
    class_pieces = lax.all_to_all(spread, "row", 0, 0, tiled=True)
    per_slot = block // chunk
    class_pieces = class_pieces.reshape(PER_CLASS, per_slot, 2, chunk, block)
    both_cols = class_pieces.transpose(2, 0, 1, 3, 4).reshape(2, PER_CLASS, block, block)
    both_rows = lax.all_gather(both_pieces, "x", axis=1, tiled=True)
    both_rows = lax.all_gather(both_rows, ("zh", "zl"), axis=1, tiled=True)
    both_rows = both_rows.reshape(2, slot_count, block, block)
    class_start = column // row_count * PER_CLASS
    row_index = target_slots[0, :, 0]
    col_index = target_slots[1, :, 0]
    present = row_index >= 0
    left_slot = jnp.clip(jnp.where(present, row_index, 0), 0, slot_count - 1)
    right_slot = jnp.clip(jnp.where(present, col_index - class_start, 0), 0, PER_CLASS - 1)
    head_live = panel_rows >= 0
    keep_head = (column == 0) & head_live[0] | (column == 1) & head_live[1]
    slots = stored.shape[0]
    keep = jnp.zeros((slots,), jnp.bool_).at[:slot_count].set(keep_head)
    panel_column = jnp.full((slots,), column == 1)
    table = jnp.stack([left_slot, right_slot, present, keep, panel_column]).astype(jnp.int32)
    rows = both_rows.reshape(2 * slot_count, block, block)
    cols = jnp.swapaxes(both_cols.reshape(2 * PER_CLASS, block, block), 1, 2)
    factored = finish_slots(table, stored, rows, cols)
    return factored[:, None]


def solution(mesh):
    row_count = mesh.shape["row"]
    col_count = mesh.shape["col"]
    devices = np.asarray(mesh.devices).reshape(
        row_count, col_count // row_count, row_count // X_SIZE, X_SIZE
    )
    split_mesh = Mesh(devices, ("row",) + COL_AXES)
    return jax.shard_map(
        per_device,
        mesh=split_mesh,
        in_specs=(
            P("row", COL_AXES, None, None),
            P(None, "row"),
            P(None, "row", COL_AXES),
            P(),
            P(),
        ),
        out_specs=P("row", COL_AXES, None, None),
        check_vma=False,
    )
```

```python
import jax
import jax.numpy as jnp
import numpy as np
from jax import lax
from jax.experimental import pallas as pl
from jax.experimental.pallas import tpu as pltpu
from jax.sharding import Mesh
from jax.sharding import PartitionSpec as P

PER_CLASS = 2
X_SIZE = 4
SLOTS_PER_STEP = 4


HIGHEST_PRECISION = lax.Precision.HIGHEST
PRODUCT_PRECISION = lax.Precision.HIGH
PLAIN_PRODUCT = (((1,), (0,)), ((), ()))
COL_AXES = ("zh", "zl", "x")
CLASS_AXES = ("zl", "x")


def apply_inverse(panel_rows_block, inverse):
    return jnp.einsum("ab,cb->ac", panel_rows_block, inverse, precision=HIGHEST_PRECISION)


def tail_kernel(table_ref, stored_ref, *refs):
    pairs = 2 * SLOTS_PER_STEP
    lefts, rights = refs[:pairs], refs[pairs:2 * pairs]
    panels, out_ref = refs[2 * pairs:2 * pairs + SLOTS_PER_STEP], refs[-1]
    step = pl.program_id(0)
    for j in range(SLOTS_PER_STEP):
        slot = step * SLOTS_PER_STEP + j
        schur = lax.dot_general(
            lefts[2 * j][0], rights[2 * j][0], PLAIN_PRODUCT, precision=PRODUCT_PRECISION,
            preferred_element_type=jnp.float32,
        )
        schur += lax.dot_general(
            lefts[2 * j + 1][0], rights[2 * j + 1][0], PLAIN_PRODUCT, precision=PRODUCT_PRECISION,
            preferred_element_type=jnp.float32,
        )
        kept = stored_ref[j] - jnp.where(table_ref[2, slot] > 0, schur, 0.0)
        out_ref[j] = jnp.where(table_ref[3, slot] > 0, panels[j][0], kept)


def finish_slots(table, stored, rows, cols):
    slots, block, _ = stored.shape
    head = rows.shape[0] // 2
    classes = cols.shape[0] // 2
    tile = (1, block, block)
    pair = (SLOTS_PER_STEP, block, block)
    left_specs = []
    right_specs = []
    panel_specs = []
    for j in range(SLOTS_PER_STEP):
        for f in range(2):
            left_specs.append(
                pl.BlockSpec(tile, lambda s, t, j=j, f=f: (f * head + t[0, s * SLOTS_PER_STEP + j], 0, 0))
            )
            right_specs.append(
                pl.BlockSpec(tile, lambda s, t, j=j, f=f: (f * classes + t[1, s * SLOTS_PER_STEP + j], 0, 0))
            )
        panel_specs.append(
            pl.BlockSpec(
                tile,
                lambda s, t, j=j: (t[4, 0] * head + jnp.minimum(s * SLOTS_PER_STEP + j, head - 1), 0, 0),
            )
        )
    spec = pltpu.PrefetchScalarGridSpec(
        num_scalar_prefetch=1,
        grid=(slots // SLOTS_PER_STEP,),
        in_specs=[pl.BlockSpec(pair, lambda s, t: (s, 0, 0))] + left_specs + right_specs + panel_specs,
        out_specs=pl.BlockSpec(pair, lambda s, t: (s, 0, 0)),
    )
    operands = [rows] * (2 * SLOTS_PER_STEP) + [cols] * (2 * SLOTS_PER_STEP) + [rows] * SLOTS_PER_STEP
    return pl.pallas_call(
        tail_kernel, grid_spec=spec, out_shape=jax.ShapeDtypeStruct(stored.shape, stored.dtype)
    )(table, stored, *operands)


def per_device(blocks, panel_rows, target_slots, diag_inverse, cross_block):
    row_count = lax.axis_size("row")
    col_count = lax.axis_size(COL_AXES)
    column = lax.axis_index(COL_AXES)
    stored = blocks[:, 0]
    slot_count = panel_rows.shape[1]
    block = stored.shape[-1]
    head_part = stored[:slot_count]
    chunk = slot_count * block // col_count
    pieces = head_part.reshape(col_count, chunk, block)
    received = lax.all_to_all(pieces, COL_AXES, 0, 0, tiled=True)
    zero_rows = received[0]
    one_rows = received[1]
    piece_slot = column * chunk // block
    first_live = lax.dynamic_index_in_dim(panel_rows[0], piece_slot, keepdims=False) >= 0
    second_live = lax.dynamic_index_in_dim(panel_rows[1], piece_slot, keepdims=False) >= 0
    cross_factor = jnp.dot(cross_block, diag_inverse[0].T, precision=HIGHEST_PRECISION)
    first_piece = jnp.where(first_live, apply_inverse(zero_rows, diag_inverse[0]), 0.0)
    updated_piece = one_rows - apply_inverse(first_piece, cross_factor)
    second_piece = jnp.where(second_live, apply_inverse(updated_piece, diag_inverse[1]), 0.0)
    both_pieces = jnp.stack([first_piece, second_piece])
    class_size = lax.axis_size(CLASS_AXES)
    swap = [(a * class_size + b, b * class_size + a) for a in range(row_count) for b in range(class_size)]
    swapped = lax.ppermute(both_pieces, ("row",) + CLASS_AXES, swap)
    spread = jnp.broadcast_to(swapped[None], (row_count,) + swapped.shape)
    class_pieces = lax.all_to_all(spread, "row", 0, 0, tiled=True)
    per_slot = block // chunk
    class_pieces = class_pieces.reshape(PER_CLASS, per_slot, 2, chunk, block)
    both_cols = class_pieces.transpose(2, 0, 1, 3, 4).reshape(2, PER_CLASS, block, block)
    both_rows = lax.all_gather(both_pieces, "x", axis=1, tiled=True)
    both_rows = lax.all_gather(both_rows, ("zh", "zl"), axis=1, tiled=True)
    both_rows = both_rows.reshape(2, slot_count, block, block)
    class_start = column // row_count * PER_CLASS
    row_index = target_slots[0, :, 0]
    col_index = target_slots[1, :, 0]
    present = row_index >= 0
    left_slot = jnp.clip(jnp.where(present, row_index, 0), 0, slot_count - 1)
    right_slot = jnp.clip(jnp.where(present, col_index - class_start, 0), 0, PER_CLASS - 1)
    head_live = panel_rows >= 0
    keep_head = (column == 0) & head_live[0] | (column == 1) & head_live[1]
    slots = stored.shape[0]
    keep = jnp.zeros((slots,), jnp.bool_).at[:slot_count].set(keep_head)
    panel_column = jnp.full((slots,), column == 1)
    table = jnp.stack([left_slot, right_slot, present, keep, panel_column]).astype(jnp.int32)
    rows = both_rows.reshape(2 * slot_count, block, block)
    cols = jnp.swapaxes(both_cols.reshape(2 * PER_CLASS, block, block), 1, 2)
    factored = finish_slots(table, stored, rows, cols)
    return factored[:, None]


def solution(mesh):
    row_count = mesh.shape["row"]
    col_count = mesh.shape["col"]
    devices = np.asarray(mesh.devices).reshape(
        row_count, col_count // row_count, row_count // X_SIZE, X_SIZE
    )
    split_mesh = Mesh(devices, ("row",) + COL_AXES)
    return jax.shard_map(
        per_device,
        mesh=split_mesh,
        in_specs=(
            P("row", COL_AXES, None, None),
            P(None, "row"),
            P(None, "row", COL_AXES),
            P(),
            P(),
        ),
        out_specs=P("row", COL_AXES, None, None),
        check_vma=False,
    )
```

```python
import jax
import jax.numpy as jnp
import numpy as np
from jax import lax
from jax.experimental import pallas as pl
from jax.experimental.pallas import tpu as pltpu
from jax.sharding import Mesh
from jax.sharding import PartitionSpec as P

PER_CLASS = 2
X_SIZE = 4
SLOTS_PER_STEP = 2


HIGHEST_PRECISION = lax.Precision.HIGHEST
PRODUCT_PRECISION = lax.Precision.HIGH
PLAIN_PRODUCT = (((1,), (0,)), ((), ()))
COL_AXES = ("zh", "zl", "x")
CLASS_AXES = ("zl", "x")


def apply_inverse(panel_rows_block, inverse):
    return jnp.einsum("ab,cb->ac", panel_rows_block, inverse, precision=HIGHEST_PRECISION)


def tail_kernel(table_ref, stored_ref, *refs):
    lefts, rights, panels, out_ref = refs[:4], refs[4:8], refs[8:10], refs[10]
    step = pl.program_id(0)
    for j in range(SLOTS_PER_STEP):
        slot = step * SLOTS_PER_STEP + j
        schur = lax.dot_general(
            lefts[2 * j][0], rights[2 * j][0], PLAIN_PRODUCT, precision=PRODUCT_PRECISION,
            preferred_element_type=jnp.float32,
        )
        schur += lax.dot_general(
            lefts[2 * j + 1][0], rights[2 * j + 1][0], PLAIN_PRODUCT, precision=PRODUCT_PRECISION,
            preferred_element_type=jnp.float32,
        )
        kept = stored_ref[j] - jnp.where(table_ref[2, slot] > 0, schur, 0.0)
        out_ref[j] = jnp.where(table_ref[3, slot] > 0, panels[j][0], kept)


def finish_slots(table, stored, rows, cols):
    slots, block, _ = stored.shape
    head = rows.shape[0] // 2
    classes = cols.shape[0] // 2
    tile = (1, block, block)
    pair = (SLOTS_PER_STEP, block, block)
    left_specs = []
    right_specs = []
    panel_specs = []
    for j in range(SLOTS_PER_STEP):
        for f in range(2):
            left_specs.append(
                pl.BlockSpec(tile, lambda s, t, j=j, f=f: (f * head + t[0, s * SLOTS_PER_STEP + j], 0, 0))
            )
            right_specs.append(
                pl.BlockSpec(tile, lambda s, t, j=j, f=f: (f * classes + t[1, s * SLOTS_PER_STEP + j], 0, 0))
            )
        panel_specs.append(
            pl.BlockSpec(
                tile,
                lambda s, t, j=j: (t[4, 0] * head + jnp.minimum(s * SLOTS_PER_STEP + j, head - 1), 0, 0),
            )
        )
    spec = pltpu.PrefetchScalarGridSpec(
        num_scalar_prefetch=1,
        grid=(slots // SLOTS_PER_STEP,),
        in_specs=[pl.BlockSpec(pair, lambda s, t: (s, 0, 0))] + left_specs + right_specs + panel_specs,
        out_specs=pl.BlockSpec(pair, lambda s, t: (s, 0, 0)),
    )
    operands = [rows] * (2 * SLOTS_PER_STEP) + [cols] * (2 * SLOTS_PER_STEP) + [rows] * SLOTS_PER_STEP
    return pl.pallas_call(
        tail_kernel, grid_spec=spec, out_shape=jax.ShapeDtypeStruct(stored.shape, stored.dtype)
    )(table, stored, *operands)


def per_device(blocks, panel_rows, target_slots, diag_inverse, cross_block):
    row_count = lax.axis_size("row")
    col_count = lax.axis_size(COL_AXES)
    column = lax.axis_index(COL_AXES)
    stored = blocks[:, 0]
    slot_count = panel_rows.shape[1]
    block = stored.shape[-1]
    head_part = stored[:slot_count]
    chunk = slot_count * block // col_count
    pieces = head_part.reshape(col_count, chunk, block)
    received = lax.all_to_all(pieces, COL_AXES, 0, 0, tiled=True)
    zero_rows = received[0]
    one_rows = received[1]
    piece_slot = column * chunk // block
    first_live = lax.dynamic_index_in_dim(panel_rows[0], piece_slot, keepdims=False) >= 0
    second_live = lax.dynamic_index_in_dim(panel_rows[1], piece_slot, keepdims=False) >= 0
    cross_factor = jnp.dot(cross_block, diag_inverse[0].T, precision=HIGHEST_PRECISION)
    first_piece = jnp.where(first_live, apply_inverse(zero_rows, diag_inverse[0]), 0.0)
    updated_piece = one_rows - apply_inverse(first_piece, cross_factor)
    second_piece = jnp.where(second_live, apply_inverse(updated_piece, diag_inverse[1]), 0.0)
    both_pieces = jnp.stack([first_piece, second_piece])
    class_size = lax.axis_size(CLASS_AXES)
    swap = [(a * class_size + b, b * class_size + a) for a in range(row_count) for b in range(class_size)]
    swapped = lax.ppermute(both_pieces, ("row",) + CLASS_AXES, swap)
    spread = jnp.broadcast_to(swapped[None], (row_count,) + swapped.shape)
    class_pieces = lax.all_to_all(spread, "row", 0, 0, tiled=True)
    per_slot = block // chunk
    class_pieces = class_pieces.reshape(PER_CLASS, per_slot, 2, chunk, block)
    both_cols = class_pieces.transpose(2, 0, 1, 3, 4).reshape(2, PER_CLASS, block, block)
    x_ring = lax.axis_size("x")
    x_place = lax.axis_index("x")
    forward = [(i, (i + 1) % x_ring) for i in range(x_ring)]
    backward = [(i, (i - 1) % x_ring) for i in range(x_ring)]
    by_offset = [both_pieces] * x_ring
    ahead = both_pieces
    behind = both_pieces
    for step in range(1, x_ring // 2 + 1):
        ahead = lax.ppermute(ahead, "x", forward)
        by_offset[x_ring - step] = ahead
        if step < x_ring - step:
            behind = lax.ppermute(behind, "x", backward)
            by_offset[step] = behind
    both_rows = jnp.roll(jnp.stack(by_offset, axis=1), x_place, axis=1)
    both_rows = both_rows.reshape(2, x_ring * chunk, block)
    both_rows = lax.all_gather(both_rows, ("zh", "zl"), axis=1, tiled=True)
    both_rows = both_rows.reshape(2, slot_count, block, block)
    class_start = column // row_count * PER_CLASS
    row_index = target_slots[0, :, 0]
    col_index = target_slots[1, :, 0]
    present = row_index >= 0
    left_slot = jnp.clip(jnp.where(present, row_index, 0), 0, slot_count - 1)
    right_slot = jnp.clip(jnp.where(present, col_index - class_start, 0), 0, PER_CLASS - 1)
    head_live = panel_rows >= 0
    keep_head = (column == 0) & head_live[0] | (column == 1) & head_live[1]
    slots = stored.shape[0]
    keep = jnp.zeros((slots,), jnp.bool_).at[:slot_count].set(keep_head)
    panel_column = jnp.full((slots,), column == 1)
    table = jnp.stack([left_slot, right_slot, present, keep, panel_column]).astype(jnp.int32)
    rows = both_rows.reshape(2 * slot_count, block, block)
    cols = jnp.swapaxes(both_cols.reshape(2 * PER_CLASS, block, block), 1, 2)
    factored = finish_slots(table, stored, rows, cols)
    return factored[:, None]


def solution(mesh):
    row_count = mesh.shape["row"]
    col_count = mesh.shape["col"]
    devices = np.asarray(mesh.devices).reshape(
        row_count, col_count // row_count, row_count // X_SIZE, X_SIZE
    )
    split_mesh = Mesh(devices, ("row",) + COL_AXES)
    return jax.shard_map(
        per_device,
        mesh=split_mesh,
        in_specs=(
            P("row", COL_AXES, None, None),
            P(None, "row"),
            P(None, "row", COL_AXES),
            P(),
            P(),
        ),
        out_specs=P("row", COL_AXES, None, None),
        check_vma=False,
    )
```

```python
import jax
import jax.numpy as jnp
import numpy as np
from jax import lax
from jax.experimental import pallas as pl
from jax.experimental.pallas import tpu as pltpu
from jax.sharding import Mesh
from jax.sharding import PartitionSpec as P

PER_CLASS = 2
X_SIZE = 4
SLOTS_PER_STEP = 2


HIGHEST_PRECISION = lax.Precision.HIGHEST
PRODUCT_PRECISION = lax.Precision.HIGH
PLAIN_PRODUCT = (((1,), (0,)), ((), ()))
COL_AXES = ("zh", "zl", "x")
CLASS_AXES = ("zl", "x")


def apply_inverse(panel_rows_block, inverse):
    return jnp.einsum("ab,cb->ac", panel_rows_block, inverse, precision=HIGHEST_PRECISION)


def tail_kernel(table_ref, stored_ref, rows_ref, cols_ref, out_ref):
    head = rows_ref.shape[0] // 2
    classes = cols_ref.shape[0] // 2
    step = pl.program_id(0)
    for j in range(SLOTS_PER_STEP):
        slot = step * SLOTS_PER_STEP + j
        left = table_ref[0, slot]
        right = table_ref[1, slot]
        schur = lax.dot_general(
            rows_ref[left], cols_ref[right], PLAIN_PRODUCT, precision=PRODUCT_PRECISION,
            preferred_element_type=jnp.float32,
        )
        schur += lax.dot_general(
            rows_ref[head + left], cols_ref[classes + right], PLAIN_PRODUCT,
            precision=PRODUCT_PRECISION, preferred_element_type=jnp.float32,
        )
        kept = stored_ref[j] - jnp.where(table_ref[2, slot] > 0, schur, 0.0)
        panel = rows_ref[table_ref[4, 0] * head + jnp.minimum(slot, head - 1)]
        out_ref[j] = jnp.where(table_ref[3, slot] > 0, panel, kept)


def finish_slots(table, stored, rows, cols):
    slots, block, _ = stored.shape
    pair = (SLOTS_PER_STEP, block, block)
    spec = pltpu.PrefetchScalarGridSpec(
        num_scalar_prefetch=1,
        grid=(slots // SLOTS_PER_STEP,),
        in_specs=[
            pl.BlockSpec(pair, lambda s, t: (s, 0, 0)),
            pl.BlockSpec(rows.shape, lambda s, t: (0, 0, 0)),
            pl.BlockSpec(cols.shape, lambda s, t: (0, 0, 0)),
        ],
        out_specs=pl.BlockSpec(pair, lambda s, t: (s, 0, 0)),
    )
    return pl.pallas_call(
        tail_kernel, grid_spec=spec, out_shape=jax.ShapeDtypeStruct(stored.shape, stored.dtype)
    )(table, stored, rows, cols)


def per_device(blocks, panel_rows, target_slots, diag_inverse, cross_block):
    row_count = lax.axis_size("row")
    col_count = lax.axis_size(COL_AXES)
    column = lax.axis_index(COL_AXES)
    stored = blocks[:, 0]
    slot_count = panel_rows.shape[1]
    block = stored.shape[-1]
    head_part = stored[:slot_count]
    chunk = slot_count * block // col_count
    pieces = head_part.reshape(col_count, chunk, block)
    received = lax.all_to_all(pieces, COL_AXES, 0, 0, tiled=True)
    zero_rows = received[0]
    one_rows = received[1]
    piece_slot = column * chunk // block
    first_live = lax.dynamic_index_in_dim(panel_rows[0], piece_slot, keepdims=False) >= 0
    second_live = lax.dynamic_index_in_dim(panel_rows[1], piece_slot, keepdims=False) >= 0
    cross_factor = jnp.dot(cross_block, diag_inverse[0].T, precision=HIGHEST_PRECISION)
    first_piece = jnp.where(first_live, apply_inverse(zero_rows, diag_inverse[0]), 0.0)
    updated_piece = one_rows - apply_inverse(first_piece, cross_factor)
    second_piece = jnp.where(second_live, apply_inverse(updated_piece, diag_inverse[1]), 0.0)
    both_pieces = jnp.stack([first_piece, second_piece])
    class_size = lax.axis_size(CLASS_AXES)
    swap = [(a * class_size + b, b * class_size + a) for a in range(row_count) for b in range(class_size)]
    swapped = lax.ppermute(both_pieces, ("row",) + CLASS_AXES, swap)
    spread = jnp.broadcast_to(swapped[None], (row_count,) + swapped.shape)
    class_pieces = lax.all_to_all(spread, "row", 0, 0, tiled=True)
    per_slot = block // chunk
    class_pieces = class_pieces.reshape(PER_CLASS, per_slot, 2, chunk, block)
    both_cols = class_pieces.transpose(2, 0, 1, 3, 4).reshape(2, PER_CLASS, block, block)
    x_ring = lax.axis_size("x")
    x_place = lax.axis_index("x")
    forward = [(i, (i + 1) % x_ring) for i in range(x_ring)]
    backward = [(i, (i - 1) % x_ring) for i in range(x_ring)]
    by_offset = [both_pieces] * x_ring
    ahead = both_pieces
    behind = both_pieces
    for step in range(1, x_ring // 2 + 1):
        ahead = lax.ppermute(ahead, "x", forward)
        by_offset[x_ring - step] = ahead
        if step < x_ring - step:
            behind = lax.ppermute(behind, "x", backward)
            by_offset[step] = behind
    both_rows = jnp.roll(jnp.stack(by_offset, axis=1), x_place, axis=1)
    both_rows = both_rows.reshape(2, x_ring * chunk, block)
    both_rows = lax.all_gather(both_rows, ("zh", "zl"), axis=1, tiled=True)
    both_rows = both_rows.reshape(2, slot_count, block, block)
    class_start = column // row_count * PER_CLASS
    row_index = target_slots[0, :, 0]
    col_index = target_slots[1, :, 0]
    present = row_index >= 0
    left_slot = jnp.clip(jnp.where(present, row_index, 0), 0, slot_count - 1)
    right_slot = jnp.clip(jnp.where(present, col_index - class_start, 0), 0, PER_CLASS - 1)
    head_live = panel_rows >= 0
    keep_head = (column == 0) & head_live[0] | (column == 1) & head_live[1]
    slots = stored.shape[0]
    keep = jnp.zeros((slots,), jnp.bool_).at[:slot_count].set(keep_head)
    panel_column = jnp.full((slots,), column == 1)
    table = jnp.stack([left_slot, right_slot, present, keep, panel_column]).astype(jnp.int32)
    rows = both_rows.reshape(2 * slot_count, block, block)
    cols = jnp.swapaxes(both_cols.reshape(2 * PER_CLASS, block, block), 1, 2)
    factored = finish_slots(table, stored, rows, cols)
    return factored[:, None]


def solution(mesh):
    row_count = mesh.shape["row"]
    col_count = mesh.shape["col"]
    devices = np.asarray(mesh.devices).reshape(
        row_count, col_count // row_count, row_count // X_SIZE, X_SIZE
    )
    split_mesh = Mesh(devices, ("row",) + COL_AXES)
    return jax.shard_map(
        per_device,
        mesh=split_mesh,
        in_specs=(
            P("row", COL_AXES, None, None),
            P(None, "row"),
            P(None, "row", COL_AXES),
            P(),
            P(),
        ),
        out_specs=P("row", COL_AXES, None, None),
        check_vma=False,
    )
```

```python
import jax
import jax.numpy as jnp
import numpy as np
from jax import lax
from jax.experimental import pallas as pl
from jax.experimental.pallas import tpu as pltpu
from jax.sharding import Mesh
from jax.sharding import PartitionSpec as P

PER_CLASS = 2
X_SIZE = 4
SLOTS_PER_STEP = 2


HIGHEST_PRECISION = lax.Precision.HIGHEST
PRODUCT_PRECISION = lax.Precision.HIGH
PLAIN_PRODUCT = (((1,), (0,)), ((), ()))
COL_AXES = ("zh", "zl", "x")
CLASS_AXES = ("zl", "x")


def apply_inverse(panel_rows_block, inverse):
    return jnp.einsum("ab,cb->ac", panel_rows_block, inverse, precision=HIGHEST_PRECISION)


def split_halves(source, high, low):
    for index in range(source.shape[0]):
        value = source[index]
        top = value.astype(jnp.bfloat16)
        high[index] = top
        low[index] = (value - top.astype(jnp.float32)).astype(jnp.bfloat16)


def three_pass(high_rows, low_rows, high_cols, low_cols, left, right):
    def dot(x, y):
        return lax.dot_general(x, y, PLAIN_PRODUCT, preferred_element_type=jnp.float32)

    top = high_rows[left]
    return dot(top, high_cols[right]) + dot(top, low_cols[right]) + dot(low_rows[left], high_cols[right])


def tail_kernel(table_ref, stored_ref, rows_ref, cols_ref, out_ref, *halves):
    high_rows, low_rows, high_cols, low_cols = halves
    head = rows_ref.shape[0] // 2
    classes = cols_ref.shape[0] // 2
    step = pl.program_id(0)

    @pl.when(step == 0)
    def _():
        split_halves(rows_ref, high_rows, low_rows)
        split_halves(cols_ref, high_cols, low_cols)

    for j in range(SLOTS_PER_STEP):
        slot = step * SLOTS_PER_STEP + j
        left = table_ref[0, slot]
        right = table_ref[1, slot]
        schur = three_pass(*halves, left, right)
        schur += three_pass(*halves, head + left, classes + right)
        kept = stored_ref[j] - jnp.where(table_ref[2, slot] > 0, schur, 0.0)
        panel = rows_ref[table_ref[4, 0] * head + jnp.minimum(slot, head - 1)]
        out_ref[j] = jnp.where(table_ref[3, slot] > 0, panel, kept)


def finish_slots(table, stored, rows, cols):
    slots, block, _ = stored.shape
    pair = (SLOTS_PER_STEP, block, block)
    spec = pltpu.PrefetchScalarGridSpec(
        num_scalar_prefetch=1,
        grid=(slots // SLOTS_PER_STEP,),
        in_specs=[
            pl.BlockSpec(pair, lambda s, t: (s, 0, 0)),
            pl.BlockSpec(rows.shape, lambda s, t: (0, 0, 0)),
            pl.BlockSpec(cols.shape, lambda s, t: (0, 0, 0)),
        ],
        out_specs=pl.BlockSpec(pair, lambda s, t: (s, 0, 0)),
        scratch_shapes=[
            pltpu.VMEM(rows.shape, jnp.bfloat16),
            pltpu.VMEM(rows.shape, jnp.bfloat16),
            pltpu.VMEM(cols.shape, jnp.bfloat16),
            pltpu.VMEM(cols.shape, jnp.bfloat16),
        ],
    )
    return pl.pallas_call(
        tail_kernel, grid_spec=spec, out_shape=jax.ShapeDtypeStruct(stored.shape, stored.dtype)
    )(table, stored, rows, cols)


def per_device(blocks, panel_rows, target_slots, diag_inverse, cross_block):
    row_count = lax.axis_size("row")
    col_count = lax.axis_size(COL_AXES)
    column = lax.axis_index(COL_AXES)
    stored = blocks[:, 0]
    slot_count = panel_rows.shape[1]
    block = stored.shape[-1]
    head_part = stored[:slot_count]
    chunk = slot_count * block // col_count
    pieces = head_part.reshape(col_count, chunk, block)
    received = lax.all_to_all(pieces, COL_AXES, 0, 0, tiled=True)
    zero_rows = received[0]
    one_rows = received[1]
    piece_slot = column * chunk // block
    first_live = lax.dynamic_index_in_dim(panel_rows[0], piece_slot, keepdims=False) >= 0
    second_live = lax.dynamic_index_in_dim(panel_rows[1], piece_slot, keepdims=False) >= 0
    cross_factor = jnp.dot(cross_block, diag_inverse[0].T, precision=HIGHEST_PRECISION)
    first_piece = jnp.where(first_live, apply_inverse(zero_rows, diag_inverse[0]), 0.0)
    updated_piece = one_rows - apply_inverse(first_piece, cross_factor)
    second_piece = jnp.where(second_live, apply_inverse(updated_piece, diag_inverse[1]), 0.0)
    both_pieces = jnp.stack([first_piece, second_piece])
    class_size = lax.axis_size(CLASS_AXES)
    swap = [(a * class_size + b, b * class_size + a) for a in range(row_count) for b in range(class_size)]
    swapped = lax.ppermute(both_pieces, ("row",) + CLASS_AXES, swap)
    spread = jnp.broadcast_to(swapped[None], (row_count,) + swapped.shape)
    class_pieces = lax.all_to_all(spread, "row", 0, 0, tiled=True)
    per_slot = block // chunk
    class_pieces = class_pieces.reshape(PER_CLASS, per_slot, 2, chunk, block)
    both_cols = class_pieces.transpose(2, 0, 1, 3, 4).reshape(2, PER_CLASS, block, block)
    x_ring = lax.axis_size("x")
    x_place = lax.axis_index("x")
    forward = [(i, (i + 1) % x_ring) for i in range(x_ring)]
    backward = [(i, (i - 1) % x_ring) for i in range(x_ring)]
    by_offset = [both_pieces] * x_ring
    ahead = both_pieces
    behind = both_pieces
    for step in range(1, x_ring // 2 + 1):
        ahead = lax.ppermute(ahead, "x", forward)
        by_offset[x_ring - step] = ahead
        if step < x_ring - step:
            behind = lax.ppermute(behind, "x", backward)
            by_offset[step] = behind
    both_rows = jnp.roll(jnp.stack(by_offset, axis=1), x_place, axis=1)
    both_rows = both_rows.reshape(2, x_ring * chunk, block)
    both_rows = lax.all_gather(both_rows, ("zh", "zl"), axis=1, tiled=True)
    both_rows = both_rows.reshape(2, slot_count, block, block)
    class_start = column // row_count * PER_CLASS
    row_index = target_slots[0, :, 0]
    col_index = target_slots[1, :, 0]
    present = row_index >= 0
    left_slot = jnp.clip(jnp.where(present, row_index, 0), 0, slot_count - 1)
    right_slot = jnp.clip(jnp.where(present, col_index - class_start, 0), 0, PER_CLASS - 1)
    head_live = panel_rows >= 0
    keep_head = (column == 0) & head_live[0] | (column == 1) & head_live[1]
    slots = stored.shape[0]
    keep = jnp.zeros((slots,), jnp.bool_).at[:slot_count].set(keep_head)
    panel_column = jnp.full((slots,), column == 1)
    table = jnp.stack([left_slot, right_slot, present, keep, panel_column]).astype(jnp.int32)
    rows = both_rows.reshape(2 * slot_count, block, block)
    cols = jnp.swapaxes(both_cols.reshape(2 * PER_CLASS, block, block), 1, 2)
    factored = finish_slots(table, stored, rows, cols)
    return factored[:, None]


def solution(mesh):
    row_count = mesh.shape["row"]
    col_count = mesh.shape["col"]
    devices = np.asarray(mesh.devices).reshape(
        row_count, col_count // row_count, row_count // X_SIZE, X_SIZE
    )
    split_mesh = Mesh(devices, ("row",) + COL_AXES)
    return jax.shard_map(
        per_device,
        mesh=split_mesh,
        in_specs=(
            P("row", COL_AXES, None, None),
            P(None, "row"),
            P(None, "row", COL_AXES),
            P(),
            P(),
        ),
        out_specs=P("row", COL_AXES, None, None),
        check_vma=False,
    )
```

```python
import jax
import jax.numpy as jnp
import numpy as np
from jax import lax
from jax.experimental import pallas as pl
from jax.experimental.pallas import tpu as pltpu
from jax.sharding import Mesh
from jax.sharding import PartitionSpec as P

PER_CLASS = 2
X_SIZE = 4
SLOTS_PER_STEP = 2


HIGHEST_PRECISION = lax.Precision.HIGHEST
PRODUCT_PRECISION = lax.Precision.HIGH
PLAIN_PRODUCT = (((1,), (0,)), ((), ()))
COL_AXES = ("zh", "zl", "x")
CLASS_AXES = ("zl", "x")


def apply_inverse(panel_rows_block, inverse):
    return jnp.einsum("ab,cb->ac", panel_rows_block, inverse, precision=HIGHEST_PRECISION)


def tail_kernel(table_ref, stored_ref, rows_ref, cols_ref, out_ref):
    head = rows_ref.shape[0] // 2
    classes = cols_ref.shape[0] // 2
    step = pl.program_id(0)
    for j in range(SLOTS_PER_STEP):
        slot = step * SLOTS_PER_STEP + j
        left = table_ref[0, slot]
        right = table_ref[1, slot]
        schur = lax.dot_general(
            rows_ref[left], cols_ref[right], PLAIN_PRODUCT, precision=PRODUCT_PRECISION,
            preferred_element_type=jnp.float32,
        )
        schur += lax.dot_general(
            rows_ref[head + left], cols_ref[classes + right], PLAIN_PRODUCT,
            precision=PRODUCT_PRECISION, preferred_element_type=jnp.float32,
        )
        kept = stored_ref[j] - jnp.where(table_ref[2, slot] > 0, schur, 0.0)
        panel = rows_ref[table_ref[4, 0] * head + jnp.minimum(slot, head - 1)]
        out_ref[j] = jnp.where(table_ref[3, slot] > 0, panel, kept)


def finish_slots(table, stored, rows, cols):
    slots, block, _ = stored.shape
    pair = (SLOTS_PER_STEP, block, block)
    spec = pltpu.PrefetchScalarGridSpec(
        num_scalar_prefetch=1,
        grid=(slots // SLOTS_PER_STEP,),
        in_specs=[
            pl.BlockSpec(pair, lambda s, t: (s, 0, 0)),
            pl.BlockSpec(rows.shape, lambda s, t: (0, 0, 0)),
            pl.BlockSpec(cols.shape, lambda s, t: (0, 0, 0)),
        ],
        out_specs=pl.BlockSpec(pair, lambda s, t: (s, 0, 0)),
    )
    return pl.pallas_call(
        tail_kernel, grid_spec=spec, out_shape=jax.ShapeDtypeStruct(stored.shape, stored.dtype)
    )(table, stored, rows, cols)


def per_device(blocks, panel_rows, target_slots, diag_inverse, cross_block):
    row_count = lax.axis_size("row")
    col_count = lax.axis_size(COL_AXES)
    column = lax.axis_index(COL_AXES)
    stored = blocks[:, 0]
    slot_count = panel_rows.shape[1]
    block = stored.shape[-1]
    head_part = stored[:slot_count]
    chunk = slot_count * block // col_count
    pieces = head_part.reshape(col_count, chunk, block)
    received = lax.all_to_all(pieces, COL_AXES, 0, 0, tiled=True)
    zero_rows = received[0]
    one_rows = received[1]
    piece_slot = column * chunk // block
    first_live = lax.dynamic_index_in_dim(panel_rows[0], piece_slot, keepdims=False) >= 0
    second_live = lax.dynamic_index_in_dim(panel_rows[1], piece_slot, keepdims=False) >= 0
    cross_factor = jnp.dot(cross_block, diag_inverse[0].T, precision=HIGHEST_PRECISION)
    first_piece = jnp.where(first_live, apply_inverse(zero_rows, diag_inverse[0]), 0.0)
    updated_piece = one_rows - apply_inverse(first_piece, cross_factor)
    second_piece = jnp.where(second_live, apply_inverse(updated_piece, diag_inverse[1]), 0.0)
    both_pieces = jnp.stack([first_piece, second_piece])
    class_size = lax.axis_size(CLASS_AXES)
    swap = [(a * class_size + b, b * class_size + a) for a in range(row_count) for b in range(class_size)]
    swapped = lax.ppermute(both_pieces, ("row",) + CLASS_AXES, swap)
    spread = jnp.broadcast_to(swapped[None], (row_count,) + swapped.shape)
    class_pieces = lax.all_to_all(spread, "row", 0, 0, tiled=True)
    per_slot = block // chunk
    class_pieces = class_pieces.reshape(PER_CLASS, per_slot, 2, chunk, block)
    both_cols = class_pieces.transpose(2, 0, 1, 3, 4).reshape(2, PER_CLASS, block, block)
    x_ring = lax.axis_size("x")
    x_place = lax.axis_index("x")
    by_offset = [both_pieces] * x_ring
    for shift in range(1, x_ring):
        pairs = [(i, (i + shift) % x_ring) for i in range(x_ring)]
        by_offset[x_ring - shift] = lax.ppermute(both_pieces, "x", pairs)
    both_rows = jnp.roll(jnp.stack(by_offset, axis=1), x_place, axis=1)
    both_rows = both_rows.reshape(2, x_ring * chunk, block)
    both_rows = lax.all_gather(both_rows, ("zh", "zl"), axis=1, tiled=True)
    both_rows = both_rows.reshape(2, slot_count, block, block)
    class_start = column // row_count * PER_CLASS
    row_index = target_slots[0, :, 0]
    col_index = target_slots[1, :, 0]
    present = row_index >= 0
    left_slot = jnp.clip(jnp.where(present, row_index, 0), 0, slot_count - 1)
    right_slot = jnp.clip(jnp.where(present, col_index - class_start, 0), 0, PER_CLASS - 1)
    head_live = panel_rows >= 0
    keep_head = (column == 0) & head_live[0] | (column == 1) & head_live[1]
    slots = stored.shape[0]
    keep = jnp.zeros((slots,), jnp.bool_).at[:slot_count].set(keep_head)
    panel_column = jnp.full((slots,), column == 1)
    table = jnp.stack([left_slot, right_slot, present, keep, panel_column]).astype(jnp.int32)
    rows = both_rows.reshape(2 * slot_count, block, block)
    cols = jnp.swapaxes(both_cols.reshape(2 * PER_CLASS, block, block), 1, 2)
    factored = finish_slots(table, stored, rows, cols)
    return factored[:, None]


def solution(mesh):
    row_count = mesh.shape["row"]
    col_count = mesh.shape["col"]
    devices = np.asarray(mesh.devices).reshape(
        row_count, col_count // row_count, row_count // X_SIZE, X_SIZE
    )
    split_mesh = Mesh(devices, ("row",) + COL_AXES)
    return jax.shard_map(
        per_device,
        mesh=split_mesh,
        in_specs=(
            P("row", COL_AXES, None, None),
            P(None, "row"),
            P(None, "row", COL_AXES),
            P(),
            P(),
        ),
        out_specs=P("row", COL_AXES, None, None),
        check_vma=False,
    )
```

```python
import jax
import jax.numpy as jnp
import numpy as np
from jax import lax
from jax.experimental import pallas as pl
from jax.experimental.pallas import tpu as pltpu
from jax.sharding import Mesh
from jax.sharding import PartitionSpec as P

PER_CLASS = 2
X_SIZE = 4
SLOTS_PER_STEP = 2


HIGHEST_PRECISION = lax.Precision.HIGHEST
PRODUCT_PRECISION = lax.Precision.HIGH
PLAIN_PRODUCT = (((1,), (0,)), ((), ()))
COL_AXES = ("zh", "zl", "x")
CLASS_AXES = ("zl", "x")


def apply_inverse(panel_rows_block, inverse):
    return jnp.einsum("ab,cb->ac", panel_rows_block, inverse, precision=PRODUCT_PRECISION)


def tail_kernel(table_ref, stored_ref, rows_ref, cols_ref, out_ref):
    head = rows_ref.shape[0] // 2
    classes = cols_ref.shape[0] // 2
    step = pl.program_id(0)
    for j in range(SLOTS_PER_STEP):
        slot = step * SLOTS_PER_STEP + j
        left = table_ref[0, slot]
        right = table_ref[1, slot]
        schur = lax.dot_general(
            rows_ref[left], cols_ref[right], PLAIN_PRODUCT, precision=PRODUCT_PRECISION,
            preferred_element_type=jnp.float32,
        )
        schur += lax.dot_general(
            rows_ref[head + left], cols_ref[classes + right], PLAIN_PRODUCT,
            precision=PRODUCT_PRECISION, preferred_element_type=jnp.float32,
        )
        kept = stored_ref[j] - jnp.where(table_ref[2, slot] > 0, schur, 0.0)
        panel = rows_ref[table_ref[4, 0] * head + jnp.minimum(slot, head - 1)]
        out_ref[j] = jnp.where(table_ref[3, slot] > 0, panel, kept)


def finish_slots(table, stored, rows, cols):
    slots, block, _ = stored.shape
    pair = (SLOTS_PER_STEP, block, block)
    spec = pltpu.PrefetchScalarGridSpec(
        num_scalar_prefetch=1,
        grid=(slots // SLOTS_PER_STEP,),
        in_specs=[
            pl.BlockSpec(pair, lambda s, t: (s, 0, 0)),
            pl.BlockSpec(rows.shape, lambda s, t: (0, 0, 0)),
            pl.BlockSpec(cols.shape, lambda s, t: (0, 0, 0)),
        ],
        out_specs=pl.BlockSpec(pair, lambda s, t: (s, 0, 0)),
    )
    return pl.pallas_call(
        tail_kernel, grid_spec=spec, out_shape=jax.ShapeDtypeStruct(stored.shape, stored.dtype)
    )(table, stored, rows, cols)


def per_device(blocks, panel_rows, target_slots, diag_inverse, cross_block):
    row_count = lax.axis_size("row")
    col_count = lax.axis_size(COL_AXES)
    column = lax.axis_index(COL_AXES)
    stored = blocks[:, 0]
    slot_count = panel_rows.shape[1]
    block = stored.shape[-1]
    head_part = stored[:slot_count]
    chunk = slot_count * block // col_count
    pieces = head_part.reshape(col_count, chunk, block)
    received = lax.all_to_all(pieces, COL_AXES, 0, 0, tiled=True)
    zero_rows = received[0]
    one_rows = received[1]
    piece_slot = column * chunk // block
    first_live = lax.dynamic_index_in_dim(panel_rows[0], piece_slot, keepdims=False) >= 0
    second_live = lax.dynamic_index_in_dim(panel_rows[1], piece_slot, keepdims=False) >= 0
    cross_factor = jnp.dot(cross_block, diag_inverse[0].T, precision=HIGHEST_PRECISION)
    first_piece = jnp.where(first_live, apply_inverse(zero_rows, diag_inverse[0]), 0.0)
    updated_piece = one_rows - apply_inverse(first_piece, cross_factor)
    second_piece = jnp.where(second_live, apply_inverse(updated_piece, diag_inverse[1]), 0.0)
    both_pieces = jnp.stack([first_piece, second_piece])
    class_size = lax.axis_size(CLASS_AXES)
    swap = [(a * class_size + b, b * class_size + a) for a in range(row_count) for b in range(class_size)]
    swapped = lax.ppermute(both_pieces, ("row",) + CLASS_AXES, swap)
    spread = jnp.broadcast_to(swapped[None], (row_count,) + swapped.shape)
    class_pieces = lax.all_to_all(spread, "row", 0, 0, tiled=True)
    per_slot = block // chunk
    class_pieces = class_pieces.reshape(PER_CLASS, per_slot, 2, chunk, block)
    both_cols = class_pieces.transpose(2, 0, 1, 3, 4).reshape(2, PER_CLASS, block, block)
    x_ring = lax.axis_size("x")
    x_place = lax.axis_index("x")
    by_offset = [both_pieces] * x_ring
    for shift in range(1, x_ring):
        pairs = [(i, (i + shift) % x_ring) for i in range(x_ring)]
        by_offset[x_ring - shift] = lax.ppermute(both_pieces, "x", pairs)
    both_rows = jnp.roll(jnp.stack(by_offset, axis=1), x_place, axis=1)
    both_rows = both_rows.reshape(2, x_ring * chunk, block)
    both_rows = lax.all_gather(both_rows, ("zh", "zl"), axis=1, tiled=True)
    both_rows = both_rows.reshape(2, slot_count, block, block)
    class_start = column // row_count * PER_CLASS
    row_index = target_slots[0, :, 0]
    col_index = target_slots[1, :, 0]
    present = row_index >= 0
    left_slot = jnp.clip(jnp.where(present, row_index, 0), 0, slot_count - 1)
    right_slot = jnp.clip(jnp.where(present, col_index - class_start, 0), 0, PER_CLASS - 1)
    head_live = panel_rows >= 0
    keep_head = (column == 0) & head_live[0] | (column == 1) & head_live[1]
    slots = stored.shape[0]
    keep = jnp.zeros((slots,), jnp.bool_).at[:slot_count].set(keep_head)
    panel_column = jnp.full((slots,), column == 1)
    table = jnp.stack([left_slot, right_slot, present, keep, panel_column]).astype(jnp.int32)
    rows = both_rows.reshape(2 * slot_count, block, block)
    cols = jnp.swapaxes(both_cols.reshape(2 * PER_CLASS, block, block), 1, 2)
    factored = finish_slots(table, stored, rows, cols)
    return factored[:, None]


def solution(mesh):
    row_count = mesh.shape["row"]
    col_count = mesh.shape["col"]
    devices = np.asarray(mesh.devices).reshape(
        row_count, col_count // row_count, row_count // X_SIZE, X_SIZE
    )
    split_mesh = Mesh(devices, ("row",) + COL_AXES)
    return jax.shard_map(
        per_device,
        mesh=split_mesh,
        in_specs=(
            P("row", COL_AXES, None, None),
            P(None, "row"),
            P(None, "row", COL_AXES),
            P(),
            P(),
        ),
        out_specs=P("row", COL_AXES, None, None),
        check_vma=False,
    )
```
